128 devices in a mesh: rows: 8 (over x, y_hi), cols: 16 (over z, y_lo, core).
Axes of the slice: x: 4, y: 4 (y_hi: 2, y_lo: 2; y = y_hi * 2 + y_lo), z: 4, core: 2. Of those that a mesh axis runs over, the one named last changes fastest.
Arguments:
- tokens: bfloat16 [256, 256, 320], P('rows', 'cols'), may hold values from -34 to 34
- norm1_gain: float32 [320], replicated, may hold values from 0.1 to 1.9
- norm1_shift: float32 [320], replicated, may hold values from -3 to 3
- w_query: bfloat16 [320, 320], replicated, may hold values from -1 to 1
- b_query: float32 [320], replicated, may hold values from -3 to 3
- w_reduce: bfloat16 [1280, 320], replicated, may hold values from -1 to 1
- b_reduce: float32 [320], replicated, may hold values from -3 to 3
- reduce_gain: float32 [320], replicated, may hold values from 0.5 to 1.5
- reduce_shift: float32 [320], replicated, may hold values from -3 to 3
- w_key: bfloat16 [320, 320], replicated, may hold values from -1 to 1
- w_value: bfloat16 [320, 320], replicated, may hold values from -0.3125 to 0.3125
- b_value: float32 [320], replicated, may hold values from -3 to 3
- w_out: bfloat16 [320, 320], replicated, may hold values from -0.75 to 0.75
- b_out: float32 [320], replicated, may hold values from -3 to 3
- norm2_gain: float32 [320], replicated, may hold values from 0.5 to 1.5
- norm2_shift: float32 [320], replicated, may hold values from -3 to 3
- w_expand: bfloat16 [320, 1280], replicated, may hold values from -0.3125 to 0.3125
- b_expand: float32 [1280], replicated, may hold values from -3 to 3
- w_depth: float32 [9, 1280], replicated, may hold values from -2 to 2
- b_depth: float32 [1280], replicated, may hold values from -3 to 3
- w_shrink: bfloat16 [1280, 320], replicated, may hold values from -0.15625 to 0.15625
- b_shrink: float32 [320], replicated, may hold values from -3 to 3
Outputs:
- block_out: bfloat16 [256, 256, 320], P('rows', 'cols')
The draws below stay inside these ranges and needn't reach their ends.
All inputs are finite; a program needn't handle non-finite values.
Results may differ from the reference program's by a relative error of at most 0.0095.
Values may be sent and summed in bfloat16 or wider, within the bound.
No kernel may reach another device: no remote copies, remote signals or barrier semaphores. Data moves between devices by JAX's collectives and lax.ppermute only.
A program may use at most 128 MiB of HBM per device.

```python
import math
import jax
import jax.numpy as jnp
from jax import lax

CH = 320
HEADS = 5
FFN_CH = 1280
GRID_ROWS = 256
GRID_COLS = 256


def draw_w_query(key, part):
    noise_key = jax.random.fold_in(key, 1)
    matrix = jnp.clip(jax.random.normal(noise_key, (CH, CH), jnp.float32), -4.0, 4.0) * 0.09
    return jnp.clip(matrix, -1.0, 1.0).astype(jnp.bfloat16)


def draw_w_key(key, part):
    noise_key = jax.random.fold_in(key, 2)
    matrix = jnp.clip(jax.random.normal(noise_key, (CH, CH), jnp.float32), -4.0, 4.0) * 0.09
    return jnp.clip(matrix, -1.0, 1.0).astype(jnp.bfloat16)


def draw_w_reduce(key, part):
    noise_key = jax.random.fold_in(key, 3)
    unit_scale = 1.0 / math.sqrt(4 * CH)
    matrix = jnp.clip(jax.random.normal(noise_key, (4 * CH, CH), jnp.float32), -4.0, 4.0) * unit_scale
    return jnp.clip(matrix, -1.0, 1.0).astype(jnp.bfloat16)


def draw_tokens(key, part):
    base = jax.random.fold_in(key, 5)
    key_one, key_two, key_three = jax.random.split(base, 3)
    shape = (GRID_ROWS, GRID_COLS, CH)
    chan_scale = jnp.exp(jax.random.uniform(key_two, (CH,), jnp.float32, -1.2, 1.2))
    place_scale = jnp.exp(jax.random.uniform(key_three, (GRID_ROWS, GRID_COLS, 1), jnp.float32, -0.7, 0.7))
    field = jnp.clip(jax.random.normal(key_one, shape, jnp.float32), -5.0, 5.0)
    result = field * chan_scale * place_scale
    return jnp.clip(result, -34.0, 34.0).astype(jnp.bfloat16)


def scatter_about(rng, shape, scale, reach, held_as=jnp.bfloat16):
    array = jax.random.normal(rng, shape, jnp.float32) * scale
    return jnp.minimum(jnp.maximum(array, -reach), reach).astype(held_as)


def setup_inputs(seed: int = 0) -> dict:
    key_list = jax.random.split(jax.random.key(seed), 23)
    tokens = draw_tokens(jax.random.fold_in(key_list[22], 71), 0)
    norm1_gain = jnp.clip(1.0 + 0.18 * jax.random.normal(key_list[1], (CH,), jnp.float32), 0.1, 1.9)
    norm1_shift = scatter_about(key_list[2], (CH,), 0.5, 3.0, jnp.float32)
    w_query = draw_w_query(jax.random.fold_in(key_list[22], 71), 0)
    b_query = scatter_about(key_list[4], (CH,), 0.5, 3.0, jnp.float32)
    w_reduce = draw_w_reduce(jax.random.fold_in(key_list[22], 71), 0)
    b_reduce = scatter_about(key_list[6], (CH,), 0.5, 3.0, jnp.float32)
    reduce_gain = jnp.clip(1.0 + 0.1 * jax.random.normal(key_list[7], (CH,), jnp.float32), 0.5, 1.5)
    reduce_shift = scatter_about(key_list[8], (CH,), 0.5, 3.0, jnp.float32)
    w_key = draw_w_key(jax.random.fold_in(key_list[22], 71), 0)
    w_value = scatter_about(key_list[10], (CH, CH), CH ** -0.5, 0.3125)
    b_value = scatter_about(key_list[11], (CH,), 0.5, 3.0, jnp.float32)
    w_out = scatter_about(key_list[12], (CH, CH), (CH / 5) ** -0.5, 0.75)
    b_out = scatter_about(key_list[13], (CH,), 0.5, 3.0, jnp.float32)
    norm2_gain = jnp.clip(1.0 + 0.1 * jax.random.normal(key_list[14], (CH,), jnp.float32), 0.5, 1.5)
    norm2_shift = scatter_about(key_list[15], (CH,), 0.5, 3.0, jnp.float32)
    w_expand = scatter_about(key_list[16], (CH, FFN_CH), CH ** -0.5, 0.3125)
    b_expand = scatter_about(key_list[17], (FFN_CH,), 0.5, 3.0, jnp.float32)
    w_depth = scatter_about(key_list[18], (9, FFN_CH), 9 ** -0.5, 2.0, jnp.float32)
    b_depth = scatter_about(key_list[19], (FFN_CH,), 0.5, 3.0, jnp.float32)
    w_shrink = scatter_about(key_list[20], (FFN_CH, CH), FFN_CH ** -0.5, 0.15625)
    b_shrink = scatter_about(key_list[21], (CH,), 0.5, 3.0, jnp.float32)
    return dict(tokens=tokens, norm1_gain=norm1_gain, norm1_shift=norm1_shift, w_query=w_query, b_query=b_query, w_reduce=w_reduce, b_reduce=b_reduce, reduce_gain=reduce_gain, reduce_shift=reduce_shift, w_key=w_key, w_value=w_value, b_value=b_value, w_out=w_out, b_out=b_out, norm2_gain=norm2_gain, norm2_shift=norm2_shift, w_expand=w_expand, b_expand=b_expand, w_depth=w_depth, b_depth=b_depth, w_shrink=w_shrink, b_shrink=b_shrink)


def layer_norm(value, gain, shift):
    mean = lax.optimization_barrier(jnp.mean(value, axis=-1, keepdims=True))
    centered = value - mean
    var = lax.optimization_barrier(jnp.mean(centered * centered, axis=-1, keepdims=True))
    return centered * lax.rsqrt(var + 1e-06) * gain + shift

def reference(tokens, norm1_gain, norm1_shift, w_query, b_query, w_reduce, b_reduce, reduce_gain, reduce_shift, w_key, w_value, b_value, w_out, b_out, norm2_gain, norm2_shift, w_expand, b_expand, w_depth, b_depth, w_shrink, b_shrink):
    grid_r, grid_c, chans = tokens.shape
    head_dim = chans // HEADS
    total = grid_r * grid_c
    flat = tokens.reshape(total, chans).astype(jnp.float32)
    normed = layer_norm(flat, norm1_gain, norm1_shift).astype(jnp.bfloat16)
    query = ((jnp.dot(normed, w_query, preferred_element_type=jnp.float32) + b_query) * head_dim ** (-0.5)).astype(jnp.bfloat16)
    query = query.reshape(total, HEADS, head_dim)
    blocks = normed.reshape(grid_r // 2, 2, grid_c // 2, 2, chans).transpose(0, 2, 1, 3, 4).reshape(-1, 4 * chans)
    reduced = jnp.dot(blocks, w_reduce, preferred_element_type=jnp.float32) + b_reduce
    reduced_norm = layer_norm(reduced, reduce_gain, reduce_shift).astype(jnp.bfloat16)
    keys = jnp.dot(reduced_norm, w_key, preferred_element_type=jnp.float32).astype(jnp.bfloat16)
    values = (jnp.dot(reduced_norm, w_value, preferred_element_type=jnp.float32) + b_value).astype(jnp.bfloat16)
    key_heads = keys.reshape(-1, HEADS, head_dim).astype(jnp.float32)
    value_heads = values.reshape(-1, HEADS, head_dim).astype(jnp.float32)
    block_len = math.gcd(total, 1024)

    def attend(query_block):
        scores = jnp.einsum('qhd,khd->hqk', query_block.astype(jnp.float32), key_heads)
        top = lax.optimization_barrier(jnp.max(scores, axis=-1, keepdims=True))
        expo = jnp.exp(scores - top)
        denom = lax.optimization_barrier(jnp.sum(expo, axis=-1))
        weight = expo.astype(jnp.bfloat16).astype(jnp.float32)
        summed = jnp.einsum('hqk,khd->hqd', weight, value_heads)
        return (summed / denom[..., None]).transpose(1, 0, 2).reshape(-1, chans)
    attended = lax.map(attend, query.reshape(total // block_len, block_len, HEADS, head_dim))
    attended = attended.reshape(total, chans).astype(jnp.bfloat16)
    mid = (flat + jnp.dot(attended, w_out, preferred_element_type=jnp.float32) + b_out).astype(jnp.bfloat16)
    normed2 = layer_norm(mid.astype(jnp.float32), norm2_gain, norm2_shift).astype(jnp.bfloat16)
    expanded = (jnp.dot(normed2, w_expand, preferred_element_type=jnp.float32) + b_expand).astype(jnp.bfloat16)
    ffn = expanded.shape[1]
    padded = jnp.pad(expanded.reshape(grid_r, grid_c, ffn), ((1, 1), (1, 1), (0, 0)))
    spread = jnp.zeros((grid_r, grid_c, ffn), jnp.float32) + b_depth
    for tap_r in range(3):
        for tap_c in range(3):
            spread = spread + padded[tap_r:tap_r + grid_r, tap_c:tap_c + grid_c, :].astype(jnp.float32) * w_depth[3 * tap_r + tap_c]
    activated = jax.nn.gelu(spread, approximate=False).astype(jnp.bfloat16).reshape(total, ffn)
    result = mid.astype(jnp.float32) + jnp.dot(activated, w_shrink, preferred_element_type=jnp.float32) + b_shrink
    return result.astype(jnp.bfloat16).reshape(grid_r, grid_c, chans)
```

```python
import jax
import jax.numpy as jnp
from jax import lax
from jax.sharding import PartitionSpec as P

HEADS = 5


def padded_2(value, sides, width):
    for axis, dim in sides:
        devices, length = (lax.axis_size(axis), value.shape[dim])
        up = [(i, (i + 1) % devices) for i in range(devices - 1)]
        down = [(j, i) for i, j in up]
        last = lax.slice_in_dim(value, length - width, length, axis=dim)
        initial = lax.slice_in_dim(value, 0, width, axis=dim)
        before = lax.ppermute(last, axis, up)
        after = lax.ppermute(initial, axis, down)
        value = jnp.concatenate([before, value, after], axis=dim)
    return value


def layer_norm(value, gain, shift):
    mean = jnp.mean(value, axis=-1, keepdims=True)
    centered = value - mean
    var = jnp.mean(centered * centered, axis=-1, keepdims=True)
    return centered * lax.rsqrt(var + 1e-06) * gain + shift


def per_device(
    tokens,
    norm1_gain,
    norm1_shift,
    w_query,
    b_query,
    w_reduce,
    b_reduce,
    reduce_gain,
    reduce_shift,
    w_key,
    w_value,
    b_value,
    w_out,
    b_out,
    norm2_gain,
    norm2_shift,
    w_expand,
    b_expand,
    w_depth,
    b_depth,
    w_shrink,
    b_shrink,
):
    tile_r, tile_c, chans = tokens.shape
    head_dim = chans // HEADS
    count = tile_r * tile_c
    flat = tokens.reshape(count, chans).astype(jnp.float32)
    normed = layer_norm(flat, norm1_gain, norm1_shift).astype(jnp.bfloat16)
    query = (
        (jnp.dot(normed, w_query, preferred_element_type=jnp.float32) + b_query)
        * head_dim ** (-0.5)
    ).astype(jnp.bfloat16)
    query = query.reshape(count, HEADS, head_dim)
    blocks = (
        normed.reshape(tile_r // 2, 2, tile_c // 2, 2, chans)
        .transpose(0, 2, 1, 3, 4)
        .reshape(-1, 4 * chans)
    )
    reduced = jnp.dot(blocks, w_reduce, preferred_element_type=jnp.float32) + b_reduce
    reduced_norm = layer_norm(reduced, reduce_gain, reduce_shift).astype(jnp.bfloat16)

    def one_block(carry, keys, values):
        run_max, run_sum, accum = carry
        key_heads = keys.reshape(-1, HEADS, head_dim)
        value_heads = values.reshape(-1, HEADS, head_dim)
        scores = jnp.einsum("qhd,khd->hqk", query, key_heads, preferred_element_type=jnp.float32)
        new_max = jnp.maximum(run_max, jnp.max(scores, axis=-1))
        factor = jnp.exp(run_max - new_max)
        expo = jnp.exp(scores - new_max[..., None])
        run_sum = run_sum * factor + jnp.sum(expo, axis=-1)
        accum = accum * factor[..., None] + jnp.einsum(
            "hqk,khd->hqd",
            expo.astype(jnp.bfloat16),
            value_heads,
            preferred_element_type=jnp.float32,
        )
        return (new_max, run_sum, accum)

    start_state = (
        jnp.full((HEADS, count), -1e30, jnp.float32),
        jnp.zeros((HEADS, count), jnp.float32),
        jnp.zeros((HEADS, count, head_dim), jnp.float32),
    )
    gathered = lax.all_gather(reduced_norm, "rows", axis=0, tiled=True)
    gathered = lax.all_gather(gathered, "cols", axis=0, tiled=True)
    attend_keys = jnp.dot(gathered, w_key, preferred_element_type=jnp.float32).astype(jnp.bfloat16)
    attend_values = (
        jnp.dot(gathered, w_value, preferred_element_type=jnp.float32) + b_value
    ).astype(jnp.bfloat16)
    carry = start_state
    length = attend_keys.shape[0]

    def step(state, pair):
        return (one_block(state, pair[0], pair[1]), None)

    carry, unused = lax.scan(
        step,
        carry,
        (
            attend_keys.reshape(length // 2048, 2048, chans),
            attend_values.reshape(length // 2048, 2048, chans),
        ),
    )
    run_max, run_sum, accum = carry
    attended = (
        (accum / run_sum[..., None]).transpose(1, 0, 2).reshape(count, chans).astype(jnp.bfloat16)
    )
    mid = (flat + jnp.dot(attended, w_out, preferred_element_type=jnp.float32) + b_out).astype(
        jnp.bfloat16
    )
    normed2 = layer_norm(mid.astype(jnp.float32), norm2_gain, norm2_shift).astype(jnp.bfloat16)
    ffn = w_expand.shape[1]
    expanded = (jnp.dot(normed2, w_expand, preferred_element_type=jnp.float32) + b_expand).astype(
        jnp.bfloat16
    )
    padded = padded_2(expanded.reshape(tile_r, tile_c, ffn), (("rows", 0), ("cols", 1)), 1)
    spread = jnp.zeros((tile_r, tile_c, ffn), jnp.float32) + b_depth
    for tap_r in range(3):
        for tap_c in range(3):
            spread = (
                spread
                + padded[tap_r : tap_r + tile_r, tap_c : tap_c + tile_c, :].astype(jnp.float32)
                * w_depth[3 * tap_r + tap_c]
            )
    activated = jax.nn.gelu(spread, approximate=False).astype(jnp.bfloat16).reshape(count, ffn)
    result = (
        mid.astype(jnp.float32)
        + jnp.dot(activated, w_shrink, preferred_element_type=jnp.float32)
        + b_shrink
    )
    return result.astype(jnp.bfloat16).reshape(tile_r, tile_c, chans)


def solution(mesh):
    placed = (
        P("rows", "cols", None),
        P(),
        P(),
        P(),
        P(),
        P(),
        P(),
        P(),
        P(),
        P(),
        P(),
        P(),
        P(),
        P(),
        P(),
        P(),
        P(),
        P(),
        P(),
        P(),
        P(),
        P(),
    )
    return jax.shard_map(
        per_device, mesh=mesh, in_specs=placed, out_specs=P("rows", "cols", None), check_vma=False
    )
```

```python
import jax
import jax.numpy as jnp
from jax import lax
from jax.sharding import PartitionSpec as P
from jax.experimental import pallas as pl
from jax.experimental.pallas import tpu as pltpu

HEADS = 5


def padded_2(value, sides, width):
    for axis, dim in sides:
        devices, length = (lax.axis_size(axis), value.shape[dim])
        up = [(i, (i + 1) % devices) for i in range(devices - 1)]
        down = [(j, i) for i, j in up]
        last = lax.slice_in_dim(value, length - width, length, axis=dim)
        initial = lax.slice_in_dim(value, 0, width, axis=dim)
        before = lax.ppermute(last, axis, up)
        after = lax.ppermute(initial, axis, down)
        value = jnp.concatenate([before, value, after], axis=dim)
    return value


def layer_norm(value, gain, shift):
    mean = jnp.mean(value, axis=-1, keepdims=True)
    centered = value - mean
    var = jnp.mean(centered * centered, axis=-1, keepdims=True)
    return centered * lax.rsqrt(var + 1e-06) * gain + shift


KV_BLOCK = 512


def attend_kernel(q_ref, rn_ref, wk_ref, wv_ref, bv_ref, o_ref, m_ref, l_ref, acc_ref):
    step = pl.program_id(0)

    @pl.when(step == 0)
    def _():
        m_ref[...] = jnp.full(m_ref.shape, -1e30, jnp.float32)
        l_ref[...] = jnp.zeros(l_ref.shape, jnp.float32)
        acc_ref[...] = jnp.zeros(acc_ref.shape, jnp.float32)

    rn = rn_ref[...]
    for h in range(HEADS):
        k_h = jnp.dot(rn, wk_ref[h], preferred_element_type=jnp.float32).astype(jnp.bfloat16)
        v_h = (jnp.dot(rn, wv_ref[h], preferred_element_type=jnp.float32) + bv_ref[h]).astype(
            jnp.bfloat16
        )
        scores = lax.dot_general(
            q_ref[h], k_h, (((1,), (1,)), ((), ())), preferred_element_type=jnp.float32
        )
        run_max = m_ref[h]
        new_max = jnp.maximum(run_max, jnp.max(scores, axis=-1, keepdims=True))
        factor = jnp.exp(run_max - new_max)
        expo = jnp.exp(scores - new_max)
        l_ref[h] = l_ref[h] * factor + jnp.sum(expo, axis=-1, keepdims=True)
        acc_ref[h] = acc_ref[h] * factor + jnp.dot(
            expo.astype(jnp.bfloat16), v_h, preferred_element_type=jnp.float32
        )
        m_ref[h] = new_max

    @pl.when(step == pl.num_programs(0) - 1)
    def _():
        o_ref[...] = (acc_ref[...] / l_ref[...]).astype(o_ref.dtype)


def attend(query_heads, gathered, wk_heads, wv_heads, bv_heads):
    heads, count, head_dim = query_heads.shape
    length, chans = gathered.shape
    return pl.pallas_call(
        attend_kernel,
        grid=(length // KV_BLOCK,),
        in_specs=[
            pl.BlockSpec((heads, count, head_dim), lambda j: (0, 0, 0)),
            pl.BlockSpec((KV_BLOCK, chans), lambda j: (j, 0)),
            pl.BlockSpec((heads, chans, head_dim), lambda j: (0, 0, 0)),
            pl.BlockSpec((heads, chans, head_dim), lambda j: (0, 0, 0)),
            pl.BlockSpec((heads, 1, head_dim), lambda j: (0, 0, 0)),
        ],
        out_specs=pl.BlockSpec((heads, count, head_dim), lambda j: (0, 0, 0)),
        out_shape=jax.ShapeDtypeStruct((heads, count, head_dim), jnp.bfloat16),
        scratch_shapes=[
            pltpu.VMEM((heads, count, 1), jnp.float32),
            pltpu.VMEM((heads, count, 1), jnp.float32),
            pltpu.VMEM((heads, count, head_dim), jnp.float32),
        ],
        compiler_params=pltpu.CompilerParams(dimension_semantics=("arbitrary",)),
    )(query_heads, gathered, wk_heads, wv_heads, bv_heads)


def per_device(
    tokens,
    norm1_gain,
    norm1_shift,
    w_query,
    b_query,
    w_reduce,
    b_reduce,
    reduce_gain,
    reduce_shift,
    w_key,
    w_value,
    b_value,
    w_out,
    b_out,
    norm2_gain,
    norm2_shift,
    w_expand,
    b_expand,
    w_depth,
    b_depth,
    w_shrink,
    b_shrink,
):
    tile_r, tile_c, chans = tokens.shape
    head_dim = chans // HEADS
    count = tile_r * tile_c
    flat = tokens.reshape(count, chans).astype(jnp.float32)
    normed = layer_norm(flat, norm1_gain, norm1_shift).astype(jnp.bfloat16)
    query = (
        (jnp.dot(normed, w_query, preferred_element_type=jnp.float32) + b_query)
        * head_dim ** (-0.5)
    ).astype(jnp.bfloat16)
    query = query.reshape(count, HEADS, head_dim)
    blocks = (
        normed.reshape(tile_r // 2, 2, tile_c // 2, 2, chans)
        .transpose(0, 2, 1, 3, 4)
        .reshape(-1, 4 * chans)
    )
    reduced = jnp.dot(blocks, w_reduce, preferred_element_type=jnp.float32) + b_reduce
    reduced_norm = layer_norm(reduced, reduce_gain, reduce_shift).astype(jnp.bfloat16)

    gathered = lax.all_gather(reduced_norm, "rows", axis=0, tiled=True)
    gathered = lax.all_gather(gathered, "cols", axis=0, tiled=True)
    wk_heads = w_key.reshape(chans, HEADS, head_dim).transpose(1, 0, 2)
    wv_heads = w_value.reshape(chans, HEADS, head_dim).transpose(1, 0, 2)
    bv_heads = b_value.reshape(HEADS, 1, head_dim)
    attended = attend(query.transpose(1, 0, 2), gathered, wk_heads, wv_heads, bv_heads)
    attended = attended.transpose(1, 0, 2).reshape(count, chans)
    mid = (flat + jnp.dot(attended, w_out, preferred_element_type=jnp.float32) + b_out).astype(
        jnp.bfloat16
    )
    normed2 = layer_norm(mid.astype(jnp.float32), norm2_gain, norm2_shift).astype(jnp.bfloat16)
    ffn = w_expand.shape[1]
    expanded = (jnp.dot(normed2, w_expand, preferred_element_type=jnp.float32) + b_expand).astype(
        jnp.bfloat16
    )
    padded = padded_2(expanded.reshape(tile_r, tile_c, ffn), (("rows", 0), ("cols", 1)), 1)
    spread = jnp.zeros((tile_r, tile_c, ffn), jnp.float32) + b_depth
    for tap_r in range(3):
        for tap_c in range(3):
            spread = (
                spread
                + padded[tap_r : tap_r + tile_r, tap_c : tap_c + tile_c, :].astype(jnp.float32)
                * w_depth[3 * tap_r + tap_c]
            )
    activated = jax.nn.gelu(spread, approximate=False).astype(jnp.bfloat16).reshape(count, ffn)
    result = (
        mid.astype(jnp.float32)
        + jnp.dot(activated, w_shrink, preferred_element_type=jnp.float32)
        + b_shrink
    )
    return result.astype(jnp.bfloat16).reshape(tile_r, tile_c, chans)


def solution(mesh):
    placed = (
        P("rows", "cols", None),
        P(),
        P(),
        P(),
        P(),
        P(),
        P(),
        P(),
        P(),
        P(),
        P(),
        P(),
        P(),
        P(),
        P(),
        P(),
        P(),
        P(),
        P(),
        P(),
        P(),
        P(),
    )
    return jax.shard_map(
        per_device, mesh=mesh, in_specs=placed, out_specs=P("rows", "cols", None), check_vma=False
    )
```

```python
import jax
import jax.numpy as jnp
from jax import lax
from jax.sharding import PartitionSpec as P
from jax.experimental import pallas as pl
from jax.experimental.pallas import tpu as pltpu

HEADS = 5


def padded_2(value, sides, width):
    for axis, dim in sides:
        devices, length = (lax.axis_size(axis), value.shape[dim])
        up = [(i, (i + 1) % devices) for i in range(devices - 1)]
        down = [(j, i) for i, j in up]
        last = lax.slice_in_dim(value, length - width, length, axis=dim)
        initial = lax.slice_in_dim(value, 0, width, axis=dim)
        before = lax.ppermute(last, axis, up)
        after = lax.ppermute(initial, axis, down)
        value = jnp.concatenate([before, value, after], axis=dim)
    return value


def layer_norm(value, gain, shift):
    mean = jnp.mean(value, axis=-1, keepdims=True)
    centered = value - mean
    var = jnp.mean(centered * centered, axis=-1, keepdims=True)
    return centered * lax.rsqrt(var + 1e-06) * gain + shift


KV_BLOCK = 4096
LANES = 128


def attend_kernel(q_ref, rn_ref, w_ref, b_ref, o_ref, m_ref, acc_ref):
    step = pl.program_id(0)
    heads, count, head_dim = o_ref.shape

    @pl.when(step == 0)
    def _():
        m_ref[...] = jnp.full(m_ref.shape, -1e30, jnp.float32)
        acc_ref[...] = jnp.zeros(acc_ref.shape, jnp.float32)

    projected = (
        jnp.dot(rn_ref[...], w_ref[...], preferred_element_type=jnp.float32) + b_ref[...]
    ).astype(jnp.bfloat16)
    for h in range(heads):
        k_h = projected[:, h * LANES : (h + 1) * LANES]
        v_h = projected[:, (heads + h) * LANES : (heads + h + 1) * LANES]
        scores = lax.dot_general(
            q_ref[h], k_h, (((1,), (1,)), ((), ())), preferred_element_type=jnp.float32
        )
        run_max = m_ref[h]
        new_max = jnp.maximum(run_max, jnp.max(scores, axis=-1, keepdims=True))
        factor = jnp.exp(run_max - new_max)
        expo = jnp.exp(scores - new_max).astype(jnp.bfloat16)
        acc_ref[h] = acc_ref[h] * factor + jnp.dot(expo, v_h, preferred_element_type=jnp.float32)
        m_ref[h] = new_max

    @pl.when(step == pl.num_programs(0) - 1)
    def _():
        acc = acc_ref[...]
        o_ref[...] = (acc[:, :, :head_dim] / acc[:, :, head_dim : head_dim + 1]).astype(o_ref.dtype)


def attend(query, gathered, w_key, w_value, b_value):
    count, chans = query.shape
    length = gathered.shape[0]
    head_dim = chans // HEADS
    spare = LANES - head_dim

    def by_head(w):
        w = w.reshape(chans, HEADS, head_dim)
        return jnp.pad(w, ((0, 0), (0, 0), (0, spare))).reshape(chans, HEADS * LANES)

    weights = jnp.concatenate([by_head(w_key), by_head(w_value)], axis=1)
    value_bias = jnp.pad(b_value.reshape(HEADS, head_dim), ((0, 0), (0, spare)))
    value_bias = value_bias.at[:, head_dim].set(1.0)
    bias = jnp.concatenate([jnp.zeros((HEADS * LANES,), jnp.float32), value_bias.reshape(-1)])
    bias = bias.reshape(1, -1)
    query_heads = jnp.pad(
        query.reshape(count, HEADS, head_dim).transpose(1, 0, 2), ((0, 0), (0, 0), (0, spare))
    )
    out = pl.pallas_call(
        attend_kernel,
        grid=(length // KV_BLOCK,),
        in_specs=[
            pl.BlockSpec((HEADS, count, LANES), lambda j: (0, 0, 0)),
            pl.BlockSpec((KV_BLOCK, chans), lambda j: (j, 0)),
            pl.BlockSpec(weights.shape, lambda j: (0, 0)),
            pl.BlockSpec(bias.shape, lambda j: (0, 0)),
        ],
        out_specs=pl.BlockSpec((HEADS, count, head_dim), lambda j: (0, 0, 0)),
        out_shape=jax.ShapeDtypeStruct((HEADS, count, head_dim), jnp.bfloat16),
        scratch_shapes=[
            pltpu.VMEM((HEADS, count, 1), jnp.float32),
            pltpu.VMEM((HEADS, count, LANES), jnp.float32),
        ],
        compiler_params=pltpu.CompilerParams(
            dimension_semantics=("arbitrary",), vmem_limit_bytes=60 * 1024 * 1024
        ),
    )(query_heads, gathered, weights, bias)
    return out.transpose(1, 0, 2).reshape(count, chans)


def per_device(
    tokens,
    norm1_gain,
    norm1_shift,
    w_query,
    b_query,
    w_reduce,
    b_reduce,
    reduce_gain,
    reduce_shift,
    w_key,
    w_value,
    b_value,
    w_out,
    b_out,
    norm2_gain,
    norm2_shift,
    w_expand,
    b_expand,
    w_depth,
    b_depth,
    w_shrink,
    b_shrink,
):
    tile_r, tile_c, chans = tokens.shape
    head_dim = chans // HEADS
    count = tile_r * tile_c
    flat = tokens.reshape(count, chans).astype(jnp.float32)
    normed = layer_norm(flat, norm1_gain, norm1_shift).astype(jnp.bfloat16)
    query = (
        (jnp.dot(normed, w_query, preferred_element_type=jnp.float32) + b_query)
        * head_dim ** (-0.5)
    ).astype(jnp.bfloat16)
    blocks = (
        normed.reshape(tile_r // 2, 2, tile_c // 2, 2, chans)
        .transpose(0, 2, 1, 3, 4)
        .reshape(-1, 4 * chans)
    )
    reduced = jnp.dot(blocks, w_reduce, preferred_element_type=jnp.float32) + b_reduce
    reduced_norm = layer_norm(reduced, reduce_gain, reduce_shift).astype(jnp.bfloat16)

    gathered = lax.all_gather(reduced_norm, "rows", axis=0, tiled=True)
    gathered = lax.all_gather(gathered, "cols", axis=0, tiled=True)
    attended = attend(query, gathered, w_key, w_value, b_value)
    mid = (flat + jnp.dot(attended, w_out, preferred_element_type=jnp.float32) + b_out).astype(
        jnp.bfloat16
    )
    normed2 = layer_norm(mid.astype(jnp.float32), norm2_gain, norm2_shift).astype(jnp.bfloat16)
    ffn = w_expand.shape[1]
    expanded = (jnp.dot(normed2, w_expand, preferred_element_type=jnp.float32) + b_expand).astype(
        jnp.bfloat16
    )
    padded = padded_2(expanded.reshape(tile_r, tile_c, ffn), (("rows", 0), ("cols", 1)), 1)
    spread = jnp.zeros((tile_r, tile_c, ffn), jnp.float32) + b_depth
    for tap_r in range(3):
        for tap_c in range(3):
            spread = (
                spread
                + padded[tap_r : tap_r + tile_r, tap_c : tap_c + tile_c, :].astype(jnp.float32)
                * w_depth[3 * tap_r + tap_c]
            )
    activated = jax.nn.gelu(spread, approximate=False).astype(jnp.bfloat16).reshape(count, ffn)
    result = (
        mid.astype(jnp.float32)
        + jnp.dot(activated, w_shrink, preferred_element_type=jnp.float32)
        + b_shrink
    )
    return result.astype(jnp.bfloat16).reshape(tile_r, tile_c, chans)


def solution(mesh):
    placed = (
        P("rows", "cols", None),
        P(),
        P(),
        P(),
        P(),
        P(),
        P(),
        P(),
        P(),
        P(),
        P(),
        P(),
        P(),
        P(),
        P(),
        P(),
        P(),
        P(),
        P(),
        P(),
        P(),
        P(),
    )
    return jax.shard_map(
        per_device, mesh=mesh, in_specs=placed, out_specs=P("rows", "cols", None), check_vma=False
    )
```

```python
import jax
import jax.numpy as jnp
from jax import lax
from jax.sharding import PartitionSpec as P
from jax.experimental import pallas as pl
from jax.experimental.pallas import tpu as pltpu

HEADS = 5


def padded_2(value, sides, width):
    for axis, dim in sides:
        devices, length = (lax.axis_size(axis), value.shape[dim])
        up = [(i, (i + 1) % devices) for i in range(devices - 1)]
        down = [(j, i) for i, j in up]
        last = lax.slice_in_dim(value, length - width, length, axis=dim)
        initial = lax.slice_in_dim(value, 0, width, axis=dim)
        before = lax.ppermute(last, axis, up)
        after = lax.ppermute(initial, axis, down)
        value = jnp.concatenate([before, value, after], axis=dim)
    return value


def gather_rows(value, axis):
    devices = lax.axis_size(axis)
    pieces = [value]
    for shift in range(1, devices):
        pairs = [(i, (i + shift) % devices) for i in range(devices)]
        pieces.append(lax.ppermute(value, axis, pairs))
    return jnp.concatenate(pieces, axis=0)


def layer_norm(value, gain, shift):
    mean = jnp.mean(value, axis=-1, keepdims=True)
    centered = value - mean
    var = jnp.mean(centered * centered, axis=-1, keepdims=True)
    return centered * lax.rsqrt(var + 1e-06) * gain + shift


KV_BLOCK = 4096
LANES = 128


def attend_kernel(q_ref, rn_ref, w_ref, b_ref, m_in_ref, acc_in_ref, m_ref, acc_ref):
    step = pl.program_id(0)
    heads = q_ref.shape[0]

    @pl.when(step == 0)
    def _():
        m_ref[...] = m_in_ref[...]
        acc_ref[...] = acc_in_ref[...]

    rn = rn_ref[...]

    def one_head(h, carry):
        projected = (
            jnp.dot(rn, w_ref[h], preferred_element_type=jnp.float32) + b_ref[h]
        ).astype(jnp.bfloat16)
        k_h = projected[:, :LANES]
        v_h = projected[:, LANES:]
        scores = lax.dot_general(
            q_ref[h], k_h, (((1,), (1,)), ((), ())), preferred_element_type=jnp.float32
        )
        run_max = m_ref[h]
        new_max = jnp.maximum(run_max, jnp.max(scores, axis=-1, keepdims=True))
        factor = jnp.exp(run_max - new_max)
        expo = jnp.exp(scores - new_max).astype(jnp.bfloat16)
        acc_ref[h] = acc_ref[h] * factor + jnp.dot(expo, v_h, preferred_element_type=jnp.float32)
        m_ref[h] = new_max
        return carry

    lax.fori_loop(0, heads, one_head, 0)


def attend_part(query_heads, part, weights, bias, run_max, accum):
    heads, count, lanes = query_heads.shape
    length, chans = part.shape
    state = pl.BlockSpec((heads, count, 1), lambda j: (0, 0, 0))
    whole = pl.BlockSpec((heads, count, lanes), lambda j: (0, 0, 0))
    return pl.pallas_call(
        attend_kernel,
        grid=(length // KV_BLOCK,),
        in_specs=[
            whole,
            pl.BlockSpec((KV_BLOCK, chans), lambda j: (j, 0)),
            pl.BlockSpec(weights.shape, lambda j: (0, 0, 0)),
            pl.BlockSpec(bias.shape, lambda j: (0, 0, 0)),
            state,
            whole,
        ],
        out_specs=[state, whole],
        out_shape=[
            jax.ShapeDtypeStruct(run_max.shape, jnp.float32),
            jax.ShapeDtypeStruct(accum.shape, jnp.float32),
        ],
        compiler_params=pltpu.CompilerParams(
            dimension_semantics=("arbitrary",), vmem_limit_bytes=60 * 1024 * 1024
        ),
    )(query_heads, part, weights, bias, run_max, accum)


def attend(query, parts, w_key, w_value, b_value):
    count, chans = query.shape
    head_dim = chans // HEADS
    spare = LANES - head_dim

    def by_head(w):
        w = w.reshape(chans, HEADS, head_dim).transpose(1, 0, 2)
        return jnp.pad(w, ((0, 0), (0, 0), (0, spare)))

    weights = jnp.concatenate([by_head(w_key), by_head(w_value)], axis=2)
    value_bias = jnp.pad(b_value.reshape(HEADS, head_dim), ((0, 0), (0, spare)))
    value_bias = value_bias.at[:, head_dim].set(1.0)
    bias = jnp.concatenate([jnp.zeros((HEADS, LANES), jnp.float32), value_bias], axis=1)
    bias = bias.reshape(HEADS, 1, 2 * LANES)
    query_heads = jnp.pad(
        query.reshape(count, HEADS, head_dim).transpose(1, 0, 2), ((0, 0), (0, 0), (0, spare))
    )
    run_max = jnp.full((HEADS, count, 1), -1e30, jnp.float32)
    accum = jnp.zeros((HEADS, count, LANES), jnp.float32)
    for part in parts:
        run_max, accum = attend_part(query_heads, part, weights, bias, run_max, accum)
    out = (accum[:, :, :head_dim] / accum[:, :, head_dim : head_dim + 1]).astype(jnp.bfloat16)
    return out.transpose(1, 0, 2).reshape(count, chans)


def per_device(
    tokens,
    norm1_gain,
    norm1_shift,
    w_query,
    b_query,
    w_reduce,
    b_reduce,
    reduce_gain,
    reduce_shift,
    w_key,
    w_value,
    b_value,
    w_out,
    b_out,
    norm2_gain,
    norm2_shift,
    w_expand,
    b_expand,
    w_depth,
    b_depth,
    w_shrink,
    b_shrink,
):
    tile_r, tile_c, chans = tokens.shape
    head_dim = chans // HEADS
    count = tile_r * tile_c
    flat = tokens.reshape(count, chans).astype(jnp.float32)
    normed = layer_norm(flat, norm1_gain, norm1_shift).astype(jnp.bfloat16)
    query = (
        (jnp.dot(normed, w_query, preferred_element_type=jnp.float32) + b_query)
        * head_dim ** (-0.5)
    ).astype(jnp.bfloat16)
    blocks = (
        normed.reshape(tile_r // 2, 2, tile_c // 2, 2, chans)
        .transpose(0, 2, 1, 3, 4)
        .reshape(-1, 4 * chans)
    )
    reduced = jnp.dot(blocks, w_reduce, preferred_element_type=jnp.float32) + b_reduce
    reduced_norm = layer_norm(reduced, reduce_gain, reduce_shift).astype(jnp.bfloat16)

    gathered = gather_rows(reduced_norm, "rows")
    half = gathered.shape[0] // 2
    parts = [
        lax.all_gather(gathered[:half], "cols", axis=0, tiled=True),
        lax.all_gather(gathered[half:], "cols", axis=0, tiled=True),
    ]
    attended = attend(query, parts, w_key, w_value, b_value)
    mid = (flat + jnp.dot(attended, w_out, preferred_element_type=jnp.float32) + b_out).astype(
        jnp.bfloat16
    )
    normed2 = layer_norm(mid.astype(jnp.float32), norm2_gain, norm2_shift).astype(jnp.bfloat16)
    ffn = w_expand.shape[1]
    expanded = (jnp.dot(normed2, w_expand, preferred_element_type=jnp.float32) + b_expand).astype(
        jnp.bfloat16
    )
    padded = padded_2(expanded.reshape(tile_r, tile_c, ffn), (("rows", 0), ("cols", 1)), 1)
    spread = jnp.zeros((tile_r, tile_c, ffn), jnp.float32) + b_depth
    for tap_r in range(3):
        for tap_c in range(3):
            spread = (
                spread
                + padded[tap_r : tap_r + tile_r, tap_c : tap_c + tile_c, :].astype(jnp.float32)
                * w_depth[3 * tap_r + tap_c]
            )
    activated = jax.nn.gelu(spread, approximate=False).astype(jnp.bfloat16).reshape(count, ffn)
    result = (
        mid.astype(jnp.float32)
        + jnp.dot(activated, w_shrink, preferred_element_type=jnp.float32)
        + b_shrink
    )
    return result.astype(jnp.bfloat16).reshape(tile_r, tile_c, chans)


def solution(mesh):
    placed = (
        P("rows", "cols", None),
        P(),
        P(),
        P(),
        P(),
        P(),
        P(),
        P(),
        P(),
        P(),
        P(),
        P(),
        P(),
        P(),
        P(),
        P(),
        P(),
        P(),
        P(),
        P(),
        P(),
        P(),
    )
    return jax.shard_map(
        per_device, mesh=mesh, in_specs=placed, out_specs=P("rows", "cols", None), check_vma=False
    )
```

```python
import jax
import jax.numpy as jnp
from jax import lax
from jax.sharding import PartitionSpec as P
from jax.experimental import pallas as pl
from jax.experimental.pallas import tpu as pltpu

HEADS = 5


def padded_2(value, sides, width):
    for axis, dim in sides:
        devices, length = (lax.axis_size(axis), value.shape[dim])
        up = [(i, (i + 1) % devices) for i in range(devices - 1)]
        down = [(j, i) for i, j in up]
        last = lax.slice_in_dim(value, length - width, length, axis=dim)
        initial = lax.slice_in_dim(value, 0, width, axis=dim)
        before = lax.ppermute(last, axis, up)
        after = lax.ppermute(initial, axis, down)
        value = jnp.concatenate([before, value, after], axis=dim)
    return value


def gather_rows(value, axis):
    devices = lax.axis_size(axis)
    pieces = [value]
    for shift in range(1, devices):
        pairs = [(i, (i + shift) % devices) for i in range(devices)]
        pieces.append(lax.ppermute(value, axis, pairs))
    return jnp.concatenate(pieces, axis=0)


def layer_norm(value, gain, shift):
    mean = jnp.mean(value, axis=-1, keepdims=True)
    centered = value - mean
    var = jnp.mean(centered * centered, axis=-1, keepdims=True)
    return centered * lax.rsqrt(var + 1e-06) * gain + shift


KV_BLOCK = 4096
LANES = 128


def attend_kernel(q_ref, rn_ref, w_ref, b_ref, m_in_ref, acc_in_ref, m_ref, acc_ref):
    step = pl.program_id(0)
    heads = q_ref.shape[0]

    @pl.when(step == 0)
    def _():
        m_ref[...] = m_in_ref[...]
        acc_ref[...] = acc_in_ref[...]

    rn = rn_ref[...]

    for h in range(heads):
        projected = (
            jnp.dot(rn, w_ref[h], preferred_element_type=jnp.float32) + b_ref[h]
        ).astype(jnp.bfloat16)
        k_h = projected[:, :LANES]
        v_h = projected[:, LANES:]
        scores = lax.dot_general(
            q_ref[h], k_h, (((1,), (1,)), ((), ())), preferred_element_type=jnp.float32
        )
        run_max = m_ref[h]
        new_max = jnp.maximum(run_max, jnp.max(scores, axis=-1, keepdims=True))
        factor = jnp.exp(run_max - new_max)
        expo = jnp.exp(scores - new_max).astype(jnp.bfloat16)
        acc_ref[h] = acc_ref[h] * factor + jnp.dot(expo, v_h, preferred_element_type=jnp.float32)
        m_ref[h] = new_max


def attend_part(query_heads, part, weights, bias, run_max, accum):
    heads, count, lanes = query_heads.shape
    length, chans = part.shape
    state = pl.BlockSpec((heads, count, 1), lambda j: (0, 0, 0))
    whole = pl.BlockSpec((heads, count, lanes), lambda j: (0, 0, 0))
    return pl.pallas_call(
        attend_kernel,
        grid=(length // KV_BLOCK,),
        in_specs=[
            whole,
            pl.BlockSpec((KV_BLOCK, chans), lambda j: (j, 0)),
            pl.BlockSpec(weights.shape, lambda j: (0, 0, 0)),
            pl.BlockSpec(bias.shape, lambda j: (0, 0, 0)),
            state,
            whole,
        ],
        out_specs=[state, whole],
        out_shape=[
            jax.ShapeDtypeStruct(run_max.shape, jnp.float32),
            jax.ShapeDtypeStruct(accum.shape, jnp.float32),
        ],
        compiler_params=pltpu.CompilerParams(
            dimension_semantics=("arbitrary",), vmem_limit_bytes=60 * 1024 * 1024
        ),
    )(query_heads, part, weights, bias, run_max, accum)


def attend(query, parts, w_key, w_value, b_value):
    count, chans = query.shape
    head_dim = chans // HEADS
    spare = LANES - head_dim

    def by_head(w):
        w = w.reshape(chans, HEADS, head_dim).transpose(1, 0, 2)
        return jnp.pad(w, ((0, 0), (0, 0), (0, spare)))

    weights = jnp.concatenate([by_head(w_key), by_head(w_value)], axis=2)
    value_bias = jnp.pad(b_value.reshape(HEADS, head_dim), ((0, 0), (0, spare)))
    value_bias = value_bias.at[:, head_dim].set(1.0)
    bias = jnp.concatenate([jnp.zeros((HEADS, LANES), jnp.float32), value_bias], axis=1)
    bias = bias.reshape(HEADS, 1, 2 * LANES)
    query_heads = jnp.pad(
        query.reshape(count, HEADS, head_dim).transpose(1, 0, 2), ((0, 0), (0, 0), (0, spare))
    )
    run_max = jnp.full((HEADS, count, 1), -1e30, jnp.float32)
    accum = jnp.zeros((HEADS, count, LANES), jnp.float32)
    for part in parts:
        run_max, accum = attend_part(query_heads, part, weights, bias, run_max, accum)
    out = (accum[:, :, :head_dim] / accum[:, :, head_dim : head_dim + 1]).astype(jnp.bfloat16)
    return out.transpose(1, 0, 2).reshape(count, chans)


def per_device(
    tokens,
    norm1_gain,
    norm1_shift,
    w_query,
    b_query,
    w_reduce,
    b_reduce,
    reduce_gain,
    reduce_shift,
    w_key,
    w_value,
    b_value,
    w_out,
    b_out,
    norm2_gain,
    norm2_shift,
    w_expand,
    b_expand,
    w_depth,
    b_depth,
    w_shrink,
    b_shrink,
):
    tile_r, tile_c, chans = tokens.shape
    head_dim = chans // HEADS
    count = tile_r * tile_c
    flat = tokens.reshape(count, chans).astype(jnp.float32)
    normed = layer_norm(flat, norm1_gain, norm1_shift).astype(jnp.bfloat16)
    query = (
        (jnp.dot(normed, w_query, preferred_element_type=jnp.float32) + b_query)
        * head_dim ** (-0.5)
    ).astype(jnp.bfloat16)
    blocks = (
        normed.reshape(tile_r // 2, 2, tile_c // 2, 2, chans)
        .transpose(0, 2, 1, 3, 4)
        .reshape(-1, 4 * chans)
    )
    reduced = jnp.dot(blocks, w_reduce, preferred_element_type=jnp.float32) + b_reduce
    reduced_norm = layer_norm(reduced, reduce_gain, reduce_shift).astype(jnp.bfloat16)

    gathered = gather_rows(reduced_norm, "rows")
    half = gathered.shape[0] // 2
    parts = [
        lax.all_gather(gathered[:half], "cols", axis=0, tiled=True),
        lax.all_gather(gathered[half:], "cols", axis=0, tiled=True),
    ]
    attended = attend(query, parts, w_key, w_value, b_value)
    mid = (flat + jnp.dot(attended, w_out, preferred_element_type=jnp.float32) + b_out).astype(
        jnp.bfloat16
    )
    normed2 = layer_norm(mid.astype(jnp.float32), norm2_gain, norm2_shift).astype(jnp.bfloat16)
    ffn = w_expand.shape[1]
    expanded = (jnp.dot(normed2, w_expand, preferred_element_type=jnp.float32) + b_expand).astype(
        jnp.bfloat16
    )
    padded = padded_2(expanded.reshape(tile_r, tile_c, ffn), (("rows", 0), ("cols", 1)), 1)
    spread = jnp.zeros((tile_r, tile_c, ffn), jnp.float32) + b_depth
    for tap_r in range(3):
        for tap_c in range(3):
            spread = (
                spread
                + padded[tap_r : tap_r + tile_r, tap_c : tap_c + tile_c, :].astype(jnp.float32)
                * w_depth[3 * tap_r + tap_c]
            )
    activated = jax.nn.gelu(spread, approximate=False).astype(jnp.bfloat16).reshape(count, ffn)
    result = (
        mid.astype(jnp.float32)
        + jnp.dot(activated, w_shrink, preferred_element_type=jnp.float32)
        + b_shrink
    )
    return result.astype(jnp.bfloat16).reshape(tile_r, tile_c, chans)


def solution(mesh):
    placed = (
        P("rows", "cols", None),
        P(),
        P(),
        P(),
        P(),
        P(),
        P(),
        P(),
        P(),
        P(),
        P(),
        P(),
        P(),
        P(),
        P(),
        P(),
        P(),
        P(),
        P(),
        P(),
        P(),
        P(),
    )
    return jax.shard_map(
        per_device, mesh=mesh, in_specs=placed, out_specs=P("rows", "cols", None), check_vma=False
    )
```

```python
import jax
import jax.numpy as jnp
from jax import lax
from jax.sharding import PartitionSpec as P
from jax.experimental import pallas as pl
from jax.experimental.pallas import tpu as pltpu

HEADS = 5


def halo(value):
    rows, cols = lax.axis_size("rows"), lax.axis_size("cols")
    grid = [(r, c) for r in range(rows) for c in range(cols)]

    def shifted(piece, dr, dc):
        pairs = [
            (r * cols + c, (r + dr) * cols + c + dc)
            for r, c in grid
            if 0 <= r + dr < rows and 0 <= c + dc < cols
        ]
        return lax.ppermute(piece, ("rows", "cols"), pairs)

    top = shifted(value[-1:], 1, 0)
    bottom = shifted(value[:1], -1, 0)
    left = shifted(value[:, -1:], 0, 1)
    right = shifted(value[:, :1], 0, -1)
    top_left = shifted(value[-1:, -1:], 1, 1)
    top_right = shifted(value[-1:, :1], 1, -1)
    bottom_left = shifted(value[:1, -1:], -1, 1)
    bottom_right = shifted(value[:1, :1], -1, -1)
    upper = jnp.concatenate([top_left, top, top_right], axis=1)
    middle = jnp.concatenate([left, value, right], axis=1)
    lower = jnp.concatenate([bottom_left, bottom, bottom_right], axis=1)
    return jnp.concatenate([upper, middle, lower], axis=0)


def gather_rows(value, axis):
    devices = lax.axis_size(axis)
    pieces = [value]
    for shift in range(1, devices):
        pairs = [(i, (i + shift) % devices) for i in range(devices)]
        pieces.append(lax.ppermute(value, axis, pairs))
    return jnp.concatenate(pieces, axis=0)


def layer_norm(value, gain, shift):
    mean = jnp.mean(value, axis=-1, keepdims=True)
    centered = value - mean
    var = jnp.mean(centered * centered, axis=-1, keepdims=True)
    return centered * lax.rsqrt(var + 1e-06) * gain + shift


KV_BLOCK = 4096
LANES = 128


def attend_kernel(q_ref, rn_ref, w_ref, b_ref, m_in_ref, acc_in_ref, m_ref, acc_ref):
    step = pl.program_id(0)
    heads = q_ref.shape[0]

    @pl.when(step == 0)
    def _():
        m_ref[...] = m_in_ref[...]
        acc_ref[...] = acc_in_ref[...]

    rn = rn_ref[...]

    def one_head(h, carry):
        projected = (
            jnp.dot(rn, w_ref[h], preferred_element_type=jnp.float32) + b_ref[h]
        ).astype(jnp.bfloat16)
        k_h = projected[:, :LANES]
        v_h = projected[:, LANES:]
        scores = lax.dot_general(
            q_ref[h], k_h, (((1,), (1,)), ((), ())), preferred_element_type=jnp.float32
        )
        run_max = m_ref[h]
        new_max = jnp.maximum(run_max, jnp.max(scores, axis=-1, keepdims=True))
        factor = jnp.exp(run_max - new_max)
        expo = jnp.exp(scores - new_max).astype(jnp.bfloat16)
        acc_ref[h] = acc_ref[h] * factor + jnp.dot(expo, v_h, preferred_element_type=jnp.float32)
        m_ref[h] = new_max
        return carry

    lax.fori_loop(0, heads, one_head, 0)


def attend_part(query_heads, part, weights, bias, run_max, accum):
    heads, count, lanes = query_heads.shape
    length, chans = part.shape
    state = pl.BlockSpec((heads, count, 1), lambda j: (0, 0, 0))
    whole = pl.BlockSpec((heads, count, lanes), lambda j: (0, 0, 0))
    return pl.pallas_call(
        attend_kernel,
        grid=(length // KV_BLOCK,),
        in_specs=[
            whole,
            pl.BlockSpec((KV_BLOCK, chans), lambda j: (j, 0)),
            pl.BlockSpec(weights.shape, lambda j: (0, 0, 0)),
            pl.BlockSpec(bias.shape, lambda j: (0, 0, 0)),
            state,
            whole,
        ],
        out_specs=[state, whole],
        out_shape=[
            jax.ShapeDtypeStruct(run_max.shape, jnp.float32),
            jax.ShapeDtypeStruct(accum.shape, jnp.float32),
        ],
        compiler_params=pltpu.CompilerParams(
            dimension_semantics=("arbitrary",), vmem_limit_bytes=60 * 1024 * 1024
        ),
    )(query_heads, part, weights, bias, run_max, accum)


def attend(query, parts, w_key, w_value, b_value):
    count, chans = query.shape
    head_dim = chans // HEADS
    spare = LANES - head_dim

    def by_head(w):
        w = w.reshape(chans, HEADS, head_dim).transpose(1, 0, 2)
        return jnp.pad(w, ((0, 0), (0, 0), (0, spare)))

    weights = jnp.concatenate([by_head(w_key), by_head(w_value)], axis=2)
    value_bias = jnp.pad(b_value.reshape(HEADS, head_dim), ((0, 0), (0, spare)))
    value_bias = value_bias.at[:, head_dim].set(1.0)
    bias = jnp.concatenate([jnp.zeros((HEADS, LANES), jnp.float32), value_bias], axis=1)
    bias = bias.reshape(HEADS, 1, 2 * LANES)
    query_heads = jnp.pad(
        query.reshape(count, HEADS, head_dim).transpose(1, 0, 2), ((0, 0), (0, 0), (0, spare))
    )
    run_max = jnp.full((HEADS, count, 1), -1e30, jnp.float32)
    accum = jnp.zeros((HEADS, count, LANES), jnp.float32)
    for part in parts:
        run_max, accum = attend_part(query_heads, part, weights, bias, run_max, accum)
    out = (accum[:, :, :head_dim] / accum[:, :, head_dim : head_dim + 1]).astype(jnp.bfloat16)
    return out.transpose(1, 0, 2).reshape(count, chans)


def per_device(
    tokens,
    norm1_gain,
    norm1_shift,
    w_query,
    b_query,
    w_reduce,
    b_reduce,
    reduce_gain,
    reduce_shift,
    w_key,
    w_value,
    b_value,
    w_out,
    b_out,
    norm2_gain,
    norm2_shift,
    w_expand,
    b_expand,
    w_depth,
    b_depth,
    w_shrink,
    b_shrink,
):
    tile_r, tile_c, chans = tokens.shape
    head_dim = chans // HEADS
    count = tile_r * tile_c
    flat = tokens.reshape(count, chans).astype(jnp.float32)
    normed = layer_norm(flat, norm1_gain, norm1_shift).astype(jnp.bfloat16)
    query = (
        (jnp.dot(normed, w_query, preferred_element_type=jnp.float32) + b_query)
        * head_dim ** (-0.5)
    ).astype(jnp.bfloat16)
    blocks = (
        normed.reshape(tile_r // 2, 2, tile_c // 2, 2, chans)
        .transpose(0, 2, 1, 3, 4)
        .reshape(-1, 4 * chans)
    )
    reduced = jnp.dot(blocks, w_reduce, preferred_element_type=jnp.float32) + b_reduce
    reduced_norm = layer_norm(reduced, reduce_gain, reduce_shift).astype(jnp.bfloat16)

    gathered = gather_rows(reduced_norm, "rows")
    half = gathered.shape[0] // 2
    parts = [
        lax.all_gather(gathered[:half], "cols", axis=0, tiled=True),
        lax.all_gather(gathered[half:], "cols", axis=0, tiled=True),
    ]
    attended = attend(query, parts, w_key, w_value, b_value)
    mid = (flat + jnp.dot(attended, w_out, preferred_element_type=jnp.float32) + b_out).astype(
        jnp.bfloat16
    )
    normed2 = layer_norm(mid.astype(jnp.float32), norm2_gain, norm2_shift).astype(jnp.bfloat16)
    ffn = w_expand.shape[1]
    expanded = (jnp.dot(normed2, w_expand, preferred_element_type=jnp.float32) + b_expand).astype(
        jnp.bfloat16
    )
    padded = halo(expanded.reshape(tile_r, tile_c, ffn))
    spread = jnp.zeros((tile_r, tile_c, ffn), jnp.float32) + b_depth
    for tap_r in range(3):
        for tap_c in range(3):
            spread = (
                spread
                + padded[tap_r : tap_r + tile_r, tap_c : tap_c + tile_c, :].astype(jnp.float32)
                * w_depth[3 * tap_r + tap_c]
            )
    activated = jax.nn.gelu(spread, approximate=False).astype(jnp.bfloat16).reshape(count, ffn)
    result = (
        mid.astype(jnp.float32)
        + jnp.dot(activated, w_shrink, preferred_element_type=jnp.float32)
        + b_shrink
    )
    return result.astype(jnp.bfloat16).reshape(tile_r, tile_c, chans)


def solution(mesh):
    placed = (
        P("rows", "cols", None),
        P(),
        P(),
        P(),
        P(),
        P(),
        P(),
        P(),
        P(),
        P(),
        P(),
        P(),
        P(),
        P(),
        P(),
        P(),
        P(),
        P(),
        P(),
        P(),
        P(),
        P(),
    )
    return jax.shard_map(
        per_device, mesh=mesh, in_specs=placed, out_specs=P("rows", "cols", None), check_vma=False
    )
```

```python
import jax
import jax.numpy as jnp
from jax import lax
from jax.sharding import PartitionSpec as P
from jax.experimental import pallas as pl
from jax.experimental.pallas import tpu as pltpu

HEADS = 5


def padded_2(value, sides, width):
    for axis, dim in sides:
        devices, length = (lax.axis_size(axis), value.shape[dim])
        up = [(i, (i + 1) % devices) for i in range(devices - 1)]
        down = [(j, i) for i, j in up]
        last = lax.slice_in_dim(value, length - width, length, axis=dim)
        initial = lax.slice_in_dim(value, 0, width, axis=dim)
        before = lax.ppermute(last, axis, up)
        after = lax.ppermute(initial, axis, down)
        value = jnp.concatenate([before, value, after], axis=dim)
    return value


def gather_rows(value, axis):
    devices = lax.axis_size(axis)
    pieces = [value]
    for shift in range(1, devices):
        pairs = [(i, (i + shift) % devices) for i in range(devices)]
        pieces.append(lax.ppermute(value, axis, pairs))
    return jnp.concatenate(pieces, axis=0)


def layer_norm(value, gain, shift):
    mean = jnp.mean(value, axis=-1, keepdims=True)
    centered = value - mean
    var = jnp.mean(centered * centered, axis=-1, keepdims=True)
    return centered * lax.rsqrt(var + 1e-06) * gain + shift


KV_BLOCK = 4096
LANES = 128


def attend_kernel(q_ref, rn_ref, w_ref, b_ref, m_in_ref, l_in_ref, acc_in_ref, m_ref, l_ref, acc_ref):
    step = pl.program_id(0)
    heads = q_ref.shape[0]
    groups = w_ref.shape[0]

    @pl.when(step == 0)
    def _():
        m_ref[...] = m_in_ref[...]
        l_ref[...] = l_in_ref[...]
        acc_ref[...] = acc_in_ref[...]

    rn = rn_ref[...]

    def one_head(h, keys, values):
        scores = lax.dot_general(
            q_ref[h], keys, (((1,), (1,)), ((), ())), preferred_element_type=jnp.float32
        )
        run_max = m_ref[h]
        new_max = jnp.maximum(run_max, jnp.max(scores, axis=-1, keepdims=True))
        factor = jnp.exp(run_max - new_max)
        expo = jnp.exp(scores - new_max)
        l_ref[h] = l_ref[h] * factor + jnp.sum(expo, axis=-1, keepdims=True)
        acc_ref[h] = acc_ref[h] * factor + jnp.dot(
            expo.astype(jnp.bfloat16), values, preferred_element_type=jnp.float32
        )
        m_ref[h] = new_max

    def project(g):
        projected = (
            jnp.dot(rn, w_ref[g], preferred_element_type=jnp.float32) + b_ref[g]
        ).astype(jnp.bfloat16)
        return projected[:, :LANES], projected[:, LANES:]

    def pair(g, carry):
        keys, values = project(g)
        one_head(2 * g, keys, values)
        one_head(2 * g + 1, keys, values)
        return carry

    lax.fori_loop(0, heads // 2, pair, 0)
    if heads % 2:
        keys, values = project(groups - 1)
        one_head(heads - 1, keys, values)


def attend_part(query_heads, part, weights, bias, state):
    heads, count, lanes = query_heads.shape
    length, chans = part.shape
    column = pl.BlockSpec((heads, count, 1), lambda j: (0, 0, 0))
    whole = pl.BlockSpec((heads, count, lanes), lambda j: (0, 0, 0))
    return pl.pallas_call(
        attend_kernel,
        grid=(length // KV_BLOCK,),
        in_specs=[
            whole,
            pl.BlockSpec((KV_BLOCK, chans), lambda j: (j, 0)),
            pl.BlockSpec(weights.shape, lambda j: (0, 0, 0)),
            pl.BlockSpec(bias.shape, lambda j: (0, 0, 0)),
            column,
            column,
            whole,
        ],
        out_specs=[column, column, whole],
        out_shape=[jax.ShapeDtypeStruct(x.shape, jnp.float32) for x in state],
        compiler_params=pltpu.CompilerParams(
            dimension_semantics=("arbitrary",), vmem_limit_bytes=60 * 1024 * 1024
        ),
    )(query_heads, part, weights, bias, *state)


def attend(query, parts, w_key, w_value, b_value):
    count, chans = query.shape
    head_dim = chans // HEADS
    groups = (HEADS + 1) // 2
    spare = 2 * groups * head_dim - chans

    def by_group(w):
        w = jnp.pad(w, ((0, 0), (0, spare)))
        return w.reshape(chans, groups, LANES).transpose(1, 0, 2)

    weights = jnp.concatenate([by_group(w_key), by_group(w_value)], axis=2)
    value_bias = jnp.pad(b_value, (0, spare)).reshape(groups, LANES)
    bias = jnp.concatenate([jnp.zeros((groups, LANES), jnp.float32), value_bias], axis=1)
    bias = bias.reshape(groups, 1, 2 * LANES)
    query_heads = query.reshape(count, HEADS, head_dim).transpose(1, 0, 2)
    odd = jnp.arange(HEADS) % 2 == 1
    query_heads = jnp.where(
        odd[:, None, None],
        jnp.pad(query_heads, ((0, 0), (0, 0), (head_dim, 0))),
        jnp.pad(query_heads, ((0, 0), (0, 0), (0, head_dim))),
    )
    state = (
        jnp.full((HEADS, count, 1), -1e30, jnp.float32),
        jnp.zeros((HEADS, count, 1), jnp.float32),
        jnp.zeros((HEADS, count, LANES), jnp.float32),
    )
    for part in parts:
        state = attend_part(query_heads, part, weights, bias, state)
    run_max, run_sum, accum = state
    accum = jnp.where(odd[:, None, None], accum[:, :, head_dim:], accum[:, :, :head_dim])
    out = (accum / run_sum).astype(jnp.bfloat16)
    return out.transpose(1, 0, 2).reshape(count, chans)


def per_device(
    tokens,
    norm1_gain,
    norm1_shift,
    w_query,
    b_query,
    w_reduce,
    b_reduce,
    reduce_gain,
    reduce_shift,
    w_key,
    w_value,
    b_value,
    w_out,
    b_out,
    norm2_gain,
    norm2_shift,
    w_expand,
    b_expand,
    w_depth,
    b_depth,
    w_shrink,
    b_shrink,
):
    tile_r, tile_c, chans = tokens.shape
    head_dim = chans // HEADS
    count = tile_r * tile_c
    flat = tokens.reshape(count, chans).astype(jnp.float32)
    normed = layer_norm(flat, norm1_gain, norm1_shift).astype(jnp.bfloat16)
    query = (
        (jnp.dot(normed, w_query, preferred_element_type=jnp.float32) + b_query)
        * head_dim ** (-0.5)
    ).astype(jnp.bfloat16)
    blocks = (
        normed.reshape(tile_r // 2, 2, tile_c // 2, 2, chans)
        .transpose(0, 2, 1, 3, 4)
        .reshape(-1, 4 * chans)
    )
    reduced = jnp.dot(blocks, w_reduce, preferred_element_type=jnp.float32) + b_reduce
    reduced_norm = layer_norm(reduced, reduce_gain, reduce_shift).astype(jnp.bfloat16)

    gathered = gather_rows(reduced_norm, "rows")
    half = gathered.shape[0] // 2
    parts = [
        lax.all_gather(gathered[:half], "cols", axis=0, tiled=True),
        lax.all_gather(gathered[half:], "cols", axis=0, tiled=True),
    ]
    attended = attend(query, parts, w_key, w_value, b_value)
    mid = (flat + jnp.dot(attended, w_out, preferred_element_type=jnp.float32) + b_out).astype(
        jnp.bfloat16
    )
    normed2 = layer_norm(mid.astype(jnp.float32), norm2_gain, norm2_shift).astype(jnp.bfloat16)
    ffn = w_expand.shape[1]
    expanded = (jnp.dot(normed2, w_expand, preferred_element_type=jnp.float32) + b_expand).astype(
        jnp.bfloat16
    )
    padded = padded_2(expanded.reshape(tile_r, tile_c, ffn), (("rows", 0), ("cols", 1)), 1)
    spread = jnp.zeros((tile_r, tile_c, ffn), jnp.float32) + b_depth
    for tap_r in range(3):
        for tap_c in range(3):
            spread = (
                spread
                + padded[tap_r : tap_r + tile_r, tap_c : tap_c + tile_c, :].astype(jnp.float32)
                * w_depth[3 * tap_r + tap_c]
            )
    activated = jax.nn.gelu(spread, approximate=False).astype(jnp.bfloat16).reshape(count, ffn)
    result = (
        mid.astype(jnp.float32)
        + jnp.dot(activated, w_shrink, preferred_element_type=jnp.float32)
        + b_shrink
    )
    return result.astype(jnp.bfloat16).reshape(tile_r, tile_c, chans)


def solution(mesh):
    placed = (
        P("rows", "cols", None),
        P(),
        P(),
        P(),
        P(),
        P(),
        P(),
        P(),
        P(),
        P(),
        P(),
        P(),
        P(),
        P(),
        P(),
        P(),
        P(),
        P(),
        P(),
        P(),
        P(),
        P(),
    )
    return jax.shard_map(
        per_device, mesh=mesh, in_specs=placed, out_specs=P("rows", "cols", None), check_vma=False
    )
```

```python
import jax
import jax.numpy as jnp
from jax import lax
from jax.sharding import PartitionSpec as P
from jax.experimental import pallas as pl
from jax.experimental.pallas import tpu as pltpu

HEADS = 5


def padded_2(value, sides, width):
    for axis, dim in sides:
        devices, length = (lax.axis_size(axis), value.shape[dim])
        up = [(i, (i + 1) % devices) for i in range(devices - 1)]
        down = [(j, i) for i, j in up]
        last = lax.slice_in_dim(value, length - width, length, axis=dim)
        initial = lax.slice_in_dim(value, 0, width, axis=dim)
        before = lax.ppermute(last, axis, up)
        after = lax.ppermute(initial, axis, down)
        value = jnp.concatenate([before, value, after], axis=dim)
    return value


def gather_rows(value, axis):
    devices = lax.axis_size(axis)
    pieces = [value]
    for shift in range(1, devices):
        pairs = [(i, (i + shift) % devices) for i in range(devices)]
        pieces.append(lax.ppermute(value, axis, pairs))
    return jnp.concatenate(pieces, axis=0)


def layer_norm(value, gain, shift):
    mean = jnp.mean(value, axis=-1, keepdims=True)
    centered = value - mean
    var = jnp.mean(centered * centered, axis=-1, keepdims=True)
    return centered * lax.rsqrt(var + 1e-06) * gain + shift


KV_BLOCK = 4096
LANES = 128


def attend_kernel(q_ref, rn_ref, w_ref, b_ref, m_in_ref, l_in_ref, acc_in_ref, m_ref, l_ref, acc_ref):
    step = pl.program_id(0)
    heads = q_ref.shape[0]
    groups = w_ref.shape[0]

    @pl.when(step == 0)
    def _():
        m_ref[...] = m_in_ref[...]
        l_ref[...] = l_in_ref[...]
        acc_ref[...] = acc_in_ref[...]

    rn = rn_ref[...]

    def one_head(h, keys, values):
        scores = lax.dot_general(
            q_ref[h], keys, (((1,), (1,)), ((), ())), preferred_element_type=jnp.float32
        )
        run_max = m_ref[h]
        new_max = jnp.maximum(run_max, jnp.max(scores, axis=-1, keepdims=True))
        factor = jnp.exp(run_max - new_max)
        expo = jnp.exp(scores - new_max)
        l_ref[h] = l_ref[h] * factor + jnp.sum(expo, axis=-1, keepdims=True)
        acc_ref[h] = acc_ref[h] * factor + jnp.dot(
            expo.astype(jnp.bfloat16), values, preferred_element_type=jnp.float32
        )
        m_ref[h] = new_max

    def project(g):
        projected = (
            jnp.dot(rn, w_ref[g], preferred_element_type=jnp.float32) + b_ref[g]
        ).astype(jnp.bfloat16)
        return projected[:, :LANES], projected[:, LANES:]

    def pair(g, carry):
        keys, values = project(g)
        one_head(2 * g, keys, values)

        @pl.when(2 * g + 1 < heads)
        def _():
            one_head(2 * g + 1, keys, values)

        return carry

    lax.fori_loop(0, groups, pair, 0)


def attend_part(query_heads, part, weights, bias, state):
    heads, count, lanes = query_heads.shape
    length, chans = part.shape
    column = pl.BlockSpec((heads, count, 1), lambda j: (0, 0, 0))
    whole = pl.BlockSpec((heads, count, lanes), lambda j: (0, 0, 0))
    return pl.pallas_call(
        attend_kernel,
        grid=(length // KV_BLOCK,),
        in_specs=[
            whole,
            pl.BlockSpec((KV_BLOCK, chans), lambda j: (j, 0)),
            pl.BlockSpec(weights.shape, lambda j: (0, 0, 0)),
            pl.BlockSpec(bias.shape, lambda j: (0, 0, 0)),
            column,
            column,
            whole,
        ],
        out_specs=[column, column, whole],
        out_shape=[jax.ShapeDtypeStruct(x.shape, jnp.float32) for x in state],
        compiler_params=pltpu.CompilerParams(
            dimension_semantics=("arbitrary",), vmem_limit_bytes=60 * 1024 * 1024
        ),
    )(query_heads, part, weights, bias, *state)


def attend(query, parts, w_key, w_value, b_value):
    count, chans = query.shape
    head_dim = chans // HEADS
    groups = (HEADS + 1) // 2
    spare = 2 * groups * head_dim - chans

    def by_group(w):
        w = jnp.pad(w, ((0, 0), (0, spare)))
        return w.reshape(chans, groups, LANES).transpose(1, 0, 2)

    weights = jnp.concatenate([by_group(w_key), by_group(w_value)], axis=2)
    value_bias = jnp.pad(b_value, (0, spare)).reshape(groups, LANES)
    bias = jnp.concatenate([jnp.zeros((groups, LANES), jnp.float32), value_bias], axis=1)
    bias = bias.reshape(groups, 1, 2 * LANES)
    query_heads = query.reshape(count, HEADS, head_dim).transpose(1, 0, 2)
    odd = jnp.arange(HEADS) % 2 == 1
    query_heads = jnp.where(
        odd[:, None, None],
        jnp.pad(query_heads, ((0, 0), (0, 0), (head_dim, 0))),
        jnp.pad(query_heads, ((0, 0), (0, 0), (0, head_dim))),
    )
    state = (
        jnp.full((HEADS, count, 1), -1e30, jnp.float32),
        jnp.zeros((HEADS, count, 1), jnp.float32),
        jnp.zeros((HEADS, count, LANES), jnp.float32),
    )
    for part in parts:
        state = attend_part(query_heads, part, weights, bias, state)
    run_max, run_sum, accum = state
    accum = jnp.where(odd[:, None, None], accum[:, :, head_dim:], accum[:, :, :head_dim])
    out = (accum / run_sum).astype(jnp.bfloat16)
    return out.transpose(1, 0, 2).reshape(count, chans)


def per_device(
    tokens,
    norm1_gain,
    norm1_shift,
    w_query,
    b_query,
    w_reduce,
    b_reduce,
    reduce_gain,
    reduce_shift,
    w_key,
    w_value,
    b_value,
    w_out,
    b_out,
    norm2_gain,
    norm2_shift,
    w_expand,
    b_expand,
    w_depth,
    b_depth,
    w_shrink,
    b_shrink,
):
    tile_r, tile_c, chans = tokens.shape
    head_dim = chans // HEADS
    count = tile_r * tile_c
    flat = tokens.reshape(count, chans).astype(jnp.float32)
    normed = layer_norm(flat, norm1_gain, norm1_shift).astype(jnp.bfloat16)
    query = (
        (jnp.dot(normed, w_query, preferred_element_type=jnp.float32) + b_query)
        * head_dim ** (-0.5)
    ).astype(jnp.bfloat16)
    blocks = (
        normed.reshape(tile_r // 2, 2, tile_c // 2, 2, chans)
        .transpose(0, 2, 1, 3, 4)
        .reshape(-1, 4 * chans)
    )
    reduced = jnp.dot(blocks, w_reduce, preferred_element_type=jnp.float32) + b_reduce
    reduced_norm = layer_norm(reduced, reduce_gain, reduce_shift).astype(jnp.bfloat16)

    gathered = gather_rows(reduced_norm, "rows")
    quarter = gathered.shape[0] // 4
    cuts = [0, quarter, 2 * quarter, gathered.shape[0]]
    parts = [
        lax.all_gather(gathered[start:stop], "cols", axis=0, tiled=True)
        for start, stop in zip(cuts[:-1], cuts[1:])
    ]
    attended = attend(query, parts, w_key, w_value, b_value)
    mid = (flat + jnp.dot(attended, w_out, preferred_element_type=jnp.float32) + b_out).astype(
        jnp.bfloat16
    )
    normed2 = layer_norm(mid.astype(jnp.float32), norm2_gain, norm2_shift).astype(jnp.bfloat16)
    ffn = w_expand.shape[1]
    expanded = (jnp.dot(normed2, w_expand, preferred_element_type=jnp.float32) + b_expand).astype(
        jnp.bfloat16
    )
    padded = padded_2(expanded.reshape(tile_r, tile_c, ffn), (("rows", 0), ("cols", 1)), 1)
    spread = jnp.zeros((tile_r, tile_c, ffn), jnp.float32) + b_depth
    for tap_r in range(3):
        for tap_c in range(3):
            spread = (
                spread
                + padded[tap_r : tap_r + tile_r, tap_c : tap_c + tile_c, :].astype(jnp.float32)
                * w_depth[3 * tap_r + tap_c]
            )
    activated = jax.nn.gelu(spread, approximate=False).astype(jnp.bfloat16).reshape(count, ffn)
    result = (
        mid.astype(jnp.float32)
        + jnp.dot(activated, w_shrink, preferred_element_type=jnp.float32)
        + b_shrink
    )
    return result.astype(jnp.bfloat16).reshape(tile_r, tile_c, chans)


def solution(mesh):
    placed = (
        P("rows", "cols", None),
        P(),
        P(),
        P(),
        P(),
        P(),
        P(),
        P(),
        P(),
        P(),
        P(),
        P(),
        P(),
        P(),
        P(),
        P(),
        P(),
        P(),
        P(),
        P(),
        P(),
        P(),
    )
    return jax.shard_map(
        per_device, mesh=mesh, in_specs=placed, out_specs=P("rows", "cols", None), check_vma=False
    )
```

```python
import jax
import jax.numpy as jnp
from jax import lax
from jax.sharding import PartitionSpec as P
from jax.experimental import pallas as pl
from jax.experimental.pallas import tpu as pltpu

HEADS = 5


def padded_2(value, sides, width):
    for axis, dim in sides:
        devices, length = (lax.axis_size(axis), value.shape[dim])
        up = [(i, (i + 1) % devices) for i in range(devices - 1)]
        down = [(j, i) for i, j in up]
        last = lax.slice_in_dim(value, length - width, length, axis=dim)
        initial = lax.slice_in_dim(value, 0, width, axis=dim)
        before = lax.ppermute(last, axis, up)
        after = lax.ppermute(initial, axis, down)
        value = jnp.concatenate([before, value, after], axis=dim)
    return value


def gather_rows(value, axis):
    devices = lax.axis_size(axis)
    if devices & (devices - 1):
        pieces = [value]
        for shift in range(1, devices):
            pairs = [(i, (i + shift) % devices) for i in range(devices)]
            pieces.append(lax.ppermute(value, axis, pairs))
        return jnp.concatenate(pieces, axis=0)
    span = 1
    while span < devices:
        pairs = [(i, i ^ span) for i in range(devices)]
        value = jnp.concatenate([value, lax.ppermute(value, axis, pairs)], axis=0)
        span *= 2
    return value


def layer_norm(value, gain, shift):
    mean = jnp.mean(value, axis=-1, keepdims=True)
    centered = value - mean
    var = jnp.mean(centered * centered, axis=-1, keepdims=True)
    return centered * lax.rsqrt(var + 1e-06) * gain + shift


KV_BLOCK = 4096
LANES = 128


def attend_kernel(q_ref, rn_ref, w_ref, b_ref, m_in_ref, l_in_ref, acc_in_ref, m_ref, l_ref, acc_ref):
    step = pl.program_id(0)
    heads = q_ref.shape[0]
    groups = w_ref.shape[0]

    @pl.when(step == 0)
    def _():
        m_ref[...] = m_in_ref[...]
        l_ref[...] = l_in_ref[...]
        acc_ref[...] = acc_in_ref[...]

    rn = rn_ref[...]

    def one_head(h, keys, values):
        scores = lax.dot_general(
            q_ref[h], keys, (((1,), (1,)), ((), ())), preferred_element_type=jnp.float32
        )
        run_max = m_ref[h]
        new_max = jnp.maximum(run_max, jnp.max(scores, axis=-1, keepdims=True))
        factor = jnp.exp(run_max - new_max)
        expo = jnp.exp(scores - new_max)
        l_ref[h] = l_ref[h] * factor + jnp.sum(expo, axis=-1, keepdims=True)
        acc_ref[h] = acc_ref[h] * factor + jnp.dot(
            expo.astype(jnp.bfloat16), values, preferred_element_type=jnp.float32
        )
        m_ref[h] = new_max

    def project(g):
        projected = (
            jnp.dot(rn, w_ref[g], preferred_element_type=jnp.float32) + b_ref[g]
        ).astype(jnp.bfloat16)
        return projected[:, :LANES], projected[:, LANES:]

    def pair(g, carry):
        keys, values = project(g)
        one_head(2 * g, keys, values)
        one_head(2 * g + 1, keys, values)
        return carry

    lax.fori_loop(0, heads // 2, pair, 0)
    if heads % 2:
        keys, values = project(groups - 1)
        one_head(heads - 1, keys, values)


def attend_part(query_heads, part, weights, bias, state):
    heads, count, lanes = query_heads.shape
    length, chans = part.shape
    column = pl.BlockSpec((heads, count, 1), lambda j: (0, 0, 0))
    whole = pl.BlockSpec((heads, count, lanes), lambda j: (0, 0, 0))
    return pl.pallas_call(
        attend_kernel,
        grid=(length // KV_BLOCK,),
        in_specs=[
            whole,
            pl.BlockSpec((KV_BLOCK, chans), lambda j: (j, 0)),
            pl.BlockSpec(weights.shape, lambda j: (0, 0, 0)),
            pl.BlockSpec(bias.shape, lambda j: (0, 0, 0)),
            column,
            column,
            whole,
        ],
        out_specs=[column, column, whole],
        out_shape=[jax.ShapeDtypeStruct(x.shape, jnp.float32) for x in state],
        compiler_params=pltpu.CompilerParams(
            dimension_semantics=("arbitrary",), vmem_limit_bytes=60 * 1024 * 1024
        ),
    )(query_heads, part, weights, bias, *state)


def attend(query, parts, w_key, w_value, b_value):
    count, chans = query.shape
    head_dim = chans // HEADS
    groups = (HEADS + 1) // 2
    spare = 2 * groups * head_dim - chans

    def by_group(w):
        w = jnp.pad(w, ((0, 0), (0, spare)))
        return w.reshape(chans, groups, LANES).transpose(1, 0, 2)

    weights = jnp.concatenate([by_group(w_key), by_group(w_value)], axis=2)
    value_bias = jnp.pad(b_value, (0, spare)).reshape(groups, LANES)
    bias = jnp.concatenate([jnp.zeros((groups, LANES), jnp.float32), value_bias], axis=1)
    bias = bias.reshape(groups, 1, 2 * LANES)
    query_heads = query.reshape(count, HEADS, head_dim).transpose(1, 0, 2)
    odd = jnp.arange(HEADS) % 2 == 1
    query_heads = jnp.where(
        odd[:, None, None],
        jnp.pad(query_heads, ((0, 0), (0, 0), (head_dim, 0))),
        jnp.pad(query_heads, ((0, 0), (0, 0), (0, head_dim))),
    )
    state = (
        jnp.full((HEADS, count, 1), -1e30, jnp.float32),
        jnp.zeros((HEADS, count, 1), jnp.float32),
        jnp.zeros((HEADS, count, LANES), jnp.float32),
    )
    for part in parts:
        state = attend_part(query_heads, part, weights, bias, state)
    run_max, run_sum, accum = state
    accum = jnp.where(odd[:, None, None], accum[:, :, head_dim:], accum[:, :, :head_dim])
    out = (accum / run_sum).astype(jnp.bfloat16)
    return out.transpose(1, 0, 2).reshape(count, chans)


def per_device(
    tokens,
    norm1_gain,
    norm1_shift,
    w_query,
    b_query,
    w_reduce,
    b_reduce,
    reduce_gain,
    reduce_shift,
    w_key,
    w_value,
    b_value,
    w_out,
    b_out,
    norm2_gain,
    norm2_shift,
    w_expand,
    b_expand,
    w_depth,
    b_depth,
    w_shrink,
    b_shrink,
):
    tile_r, tile_c, chans = tokens.shape
    head_dim = chans // HEADS
    count = tile_r * tile_c
    flat = tokens.reshape(count, chans).astype(jnp.float32)
    normed = layer_norm(flat, norm1_gain, norm1_shift).astype(jnp.bfloat16)
    query = (
        (jnp.dot(normed, w_query, preferred_element_type=jnp.float32) + b_query)
        * head_dim ** (-0.5)
    ).astype(jnp.bfloat16)
    blocks = (
        normed.reshape(tile_r // 2, 2, tile_c // 2, 2, chans)
        .transpose(0, 2, 1, 3, 4)
        .reshape(-1, 4 * chans)
    )
    reduced = jnp.dot(blocks, w_reduce, preferred_element_type=jnp.float32) + b_reduce
    reduced_norm = layer_norm(reduced, reduce_gain, reduce_shift).astype(jnp.bfloat16)

    gathered = gather_rows(reduced_norm, "rows")
    half = gathered.shape[0] // 2
    parts = [
        lax.all_gather(gathered[:half], "cols", axis=0, tiled=True),
        lax.all_gather(gathered[half:], "cols", axis=0, tiled=True),
    ]
    attended = attend(query, parts, w_key, w_value, b_value)
    mid = (flat + jnp.dot(attended, w_out, preferred_element_type=jnp.float32) + b_out).astype(
        jnp.bfloat16
    )
    normed2 = layer_norm(mid.astype(jnp.float32), norm2_gain, norm2_shift).astype(jnp.bfloat16)
    ffn = w_expand.shape[1]
    expanded = (jnp.dot(normed2, w_expand, preferred_element_type=jnp.float32) + b_expand).astype(
        jnp.bfloat16
    )
    padded = padded_2(expanded.reshape(tile_r, tile_c, ffn), (("rows", 0), ("cols", 1)), 1)
    spread = jnp.zeros((tile_r, tile_c, ffn), jnp.float32) + b_depth
    for tap_r in range(3):
        for tap_c in range(3):
            spread = (
                spread
                + padded[tap_r : tap_r + tile_r, tap_c : tap_c + tile_c, :].astype(jnp.float32)
                * w_depth[3 * tap_r + tap_c]
            )
    activated = jax.nn.gelu(spread, approximate=False).astype(jnp.bfloat16).reshape(count, ffn)
    result = (
        mid.astype(jnp.float32)
        + jnp.dot(activated, w_shrink, preferred_element_type=jnp.float32)
        + b_shrink
    )
    return result.astype(jnp.bfloat16).reshape(tile_r, tile_c, chans)


def solution(mesh):
    placed = (
        P("rows", "cols", None),
        P(),
        P(),
        P(),
        P(),
        P(),
        P(),
        P(),
        P(),
        P(),
        P(),
        P(),
        P(),
        P(),
        P(),
        P(),
        P(),
        P(),
        P(),
        P(),
        P(),
        P(),
    )
    return jax.shard_map(
        per_device, mesh=mesh, in_specs=placed, out_specs=P("rows", "cols", None), check_vma=False
    )
```

```python
import jax
import jax.numpy as jnp
from jax import lax
from jax.sharding import PartitionSpec as P
from jax.experimental import pallas as pl
from jax.experimental.pallas import tpu as pltpu

HEADS = 5


def padded_2(value, sides, width):
    for axis, dim in sides:
        devices, length = (lax.axis_size(axis), value.shape[dim])
        up = [(i, (i + 1) % devices) for i in range(devices - 1)]
        down = [(j, i) for i, j in up]
        last = lax.slice_in_dim(value, length - width, length, axis=dim)
        initial = lax.slice_in_dim(value, 0, width, axis=dim)
        before = lax.ppermute(last, axis, up)
        after = lax.ppermute(initial, axis, down)
        value = jnp.concatenate([before, value, after], axis=dim)
    return value


def gather_rows(value, axis):
    devices = lax.axis_size(axis)
    pieces = [value]
    for shift in range(1, devices):
        pairs = [(i, (i + shift) % devices) for i in range(devices)]
        pieces.append(lax.ppermute(value, axis, pairs))
    return jnp.concatenate(pieces, axis=0)


def layer_norm(value, gain, shift):
    mean = jnp.mean(value, axis=-1, keepdims=True)
    centered = value - mean
    var = jnp.mean(centered * centered, axis=-1, keepdims=True)
    return centered * lax.rsqrt(var + 1e-06) * gain + shift


KV_BLOCK = 4096
LANES = 128


def attend_kernel(q_ref, rn_ref, w_ref, b_ref, m_in_ref, l_in_ref, acc_in_ref, m_ref, l_ref, acc_ref):
    step = pl.program_id(0)
    heads = q_ref.shape[0]
    groups = w_ref.shape[0]

    @pl.when(step == 0)
    def _():
        m_ref[...] = m_in_ref[...]
        l_ref[...] = l_in_ref[...]
        acc_ref[...] = acc_in_ref[...]

    rn = rn_ref[...]

    def one_head(h, keys, values):
        scores = lax.dot_general(
            q_ref[h], keys, (((1,), (1,)), ((), ())), preferred_element_type=jnp.float32
        )
        run_max = m_ref[h]
        new_max = jnp.maximum(run_max, jnp.max(scores, axis=-1, keepdims=True))
        factor = jnp.exp(run_max - new_max)
        expo = jnp.exp(scores - new_max)
        l_ref[h] = l_ref[h] * factor + jnp.sum(expo, axis=-1, keepdims=True)
        acc_ref[h] = acc_ref[h] * factor + jnp.dot(
            expo.astype(jnp.bfloat16), values, preferred_element_type=jnp.float32
        )
        m_ref[h] = new_max

    def project(g):
        projected = (
            jnp.dot(rn, w_ref[g], preferred_element_type=jnp.float32) + b_ref[g]
        ).astype(jnp.bfloat16)
        return projected[:, :LANES], projected[:, LANES:]

    def pair(g, carry):
        keys, values = project(g)
        one_head(2 * g, keys, values)
        one_head(2 * g + 1, keys, values)
        return carry

    lax.fori_loop(0, heads // 2, pair, 0)
    if heads % 2:
        keys, values = project(groups - 1)
        one_head(heads - 1, keys, values)


def attend_part(query_heads, part, weights, bias, state):
    heads, count, lanes = query_heads.shape
    length, chans = part.shape
    column = pl.BlockSpec((heads, count, 1), lambda j: (0, 0, 0))
    whole = pl.BlockSpec((heads, count, lanes), lambda j: (0, 0, 0))
    return pl.pallas_call(
        attend_kernel,
        grid=(length // KV_BLOCK,),
        in_specs=[
            whole,
            pl.BlockSpec((KV_BLOCK, chans), lambda j: (j, 0)),
            pl.BlockSpec(weights.shape, lambda j: (0, 0, 0)),
            pl.BlockSpec(bias.shape, lambda j: (0, 0, 0)),
            column,
            column,
            whole,
        ],
        out_specs=[column, column, whole],
        out_shape=[jax.ShapeDtypeStruct(x.shape, jnp.float32) for x in state],
        compiler_params=pltpu.CompilerParams(
            dimension_semantics=("arbitrary",), vmem_limit_bytes=60 * 1024 * 1024
        ),
    )(query_heads, part, weights, bias, *state)


def attend(query, parts, w_key, w_value, b_value):
    count, chans = query.shape
    head_dim = chans // HEADS
    groups = (HEADS + 1) // 2
    spare = 2 * groups * head_dim - chans

    def by_group(w):
        w = jnp.pad(w, ((0, 0), (0, spare)))
        return w.reshape(chans, groups, LANES).transpose(1, 0, 2)

    weights = jnp.concatenate([by_group(w_key), by_group(w_value)], axis=2)
    value_bias = jnp.pad(b_value, (0, spare)).reshape(groups, LANES)
    bias = jnp.concatenate([jnp.zeros((groups, LANES), jnp.float32), value_bias], axis=1)
    bias = bias.reshape(groups, 1, 2 * LANES)
    query_heads = query.reshape(count, HEADS, head_dim).transpose(1, 0, 2)
    odd = jnp.arange(HEADS) % 2 == 1
    query_heads = jnp.where(
        odd[:, None, None],
        jnp.pad(query_heads, ((0, 0), (0, 0), (head_dim, 0))),
        jnp.pad(query_heads, ((0, 0), (0, 0), (0, head_dim))),
    )
    state = (
        jnp.full((HEADS, count, 1), -1e30, jnp.float32),
        jnp.zeros((HEADS, count, 1), jnp.float32),
        jnp.zeros((HEADS, count, LANES), jnp.float32),
    )
    for part in parts:
        state = attend_part(query_heads, part, weights, bias, state)
    run_max, run_sum, accum = state
    accum = jnp.where(odd[:, None, None], accum[:, :, head_dim:], accum[:, :, :head_dim])
    out = (accum / run_sum).astype(jnp.bfloat16)
    return out.transpose(1, 0, 2).reshape(count, chans)


def per_device(
    tokens,
    norm1_gain,
    norm1_shift,
    w_query,
    b_query,
    w_reduce,
    b_reduce,
    reduce_gain,
    reduce_shift,
    w_key,
    w_value,
    b_value,
    w_out,
    b_out,
    norm2_gain,
    norm2_shift,
    w_expand,
    b_expand,
    w_depth,
    b_depth,
    w_shrink,
    b_shrink,
):
    tile_r, tile_c, chans = tokens.shape
    head_dim = chans // HEADS
    count = tile_r * tile_c
    flat = tokens.reshape(count, chans).astype(jnp.float32)
    normed = layer_norm(flat, norm1_gain, norm1_shift).astype(jnp.bfloat16)
    query = (
        (jnp.dot(normed, w_query, preferred_element_type=jnp.float32) + b_query)
        * head_dim ** (-0.5)
    ).astype(jnp.bfloat16)
    blocks = (
        normed.reshape(tile_r // 2, 2, tile_c // 2, 2, chans)
        .transpose(0, 2, 1, 3, 4)
        .reshape(-1, 4 * chans)
    )
    reduced = jnp.dot(blocks, w_reduce, preferred_element_type=jnp.float32) + b_reduce
    reduced_norm = layer_norm(reduced, reduce_gain, reduce_shift).astype(jnp.bfloat16)

    gathered = gather_rows(reduced_norm, "rows")
    half = gathered.shape[0] // 2
    parts = [
        lax.all_gather(gathered[:half], "cols", axis=0, tiled=True),
        lax.all_gather(gathered[half:], "cols", axis=0, tiled=True),
    ]
    attended = attend(query, parts, w_key, w_value, b_value)
    mid = (flat + jnp.dot(attended, w_out, preferred_element_type=jnp.float32) + b_out).astype(
        jnp.bfloat16
    )
    normed2 = layer_norm(mid.astype(jnp.float32), norm2_gain, norm2_shift).astype(jnp.bfloat16)
    ffn = w_expand.shape[1]
    expanded = (jnp.dot(normed2, w_expand, preferred_element_type=jnp.float32) + b_expand).astype(
        jnp.bfloat16
    )
    grid = expanded.reshape(tile_r, tile_c, ffn)

    def depthwise(source, out_r, out_c):
        total = 0.0
        for tap_r in range(3):
            for tap_c in range(3):
                total = total + (
                    source[tap_r : tap_r + out_r, tap_c : tap_c + out_c, :].astype(jnp.float32)
                    * w_depth[3 * tap_r + tap_c]
                )
        return total

    local = jnp.pad(grid, ((1, 1), (1, 1), (0, 0)))
    spread = lax.optimization_barrier(depthwise(local, tile_r, tile_c) + b_depth)
    padded = padded_2(grid, (("rows", 0), ("cols", 1)), 1)
    ring = padded.at[1 : tile_r + 1, 1 : tile_c + 1, :].set(0)
    top = depthwise(ring[0:3], 1, tile_c)
    bottom = depthwise(ring[tile_r - 1 : tile_r + 2], 1, tile_c)
    left = depthwise(ring[1 : tile_r + 1, 0:3], tile_r - 2, 1)
    right = depthwise(ring[1 : tile_r + 1, tile_c - 1 : tile_c + 2], tile_r - 2, 1)
    spread = spread.at[0:1].add(top).at[tile_r - 1 : tile_r].add(bottom)
    spread = spread.at[1 : tile_r - 1, 0:1].add(left).at[1 : tile_r - 1, tile_c - 1 : tile_c].add(right)
    activated = jax.nn.gelu(spread, approximate=False).astype(jnp.bfloat16).reshape(count, ffn)
    result = (
        mid.astype(jnp.float32)
        + jnp.dot(activated, w_shrink, preferred_element_type=jnp.float32)
        + b_shrink
    )
    return result.astype(jnp.bfloat16).reshape(tile_r, tile_c, chans)


def solution(mesh):
    placed = (
        P("rows", "cols", None),
        P(),
        P(),
        P(),
        P(),
        P(),
        P(),
        P(),
        P(),
        P(),
        P(),
        P(),
        P(),
        P(),
        P(),
        P(),
        P(),
        P(),
        P(),
        P(),
        P(),
        P(),
    )
    return jax.shard_map(
        per_device, mesh=mesh, in_specs=placed, out_specs=P("rows", "cols", None), check_vma=False
    )
```

```python
import jax
import numpy as np
import jax.numpy as jnp
from jax import lax
from jax.sharding import PartitionSpec as P
from jax.experimental import pallas as pl
from jax.experimental.pallas import tpu as pltpu

HEADS = 5


def padded_2(value, sides, width):
    for axis, dim in sides:
        devices, length = (lax.axis_size(axis), value.shape[dim])
        up = [(i, (i + 1) % devices) for i in range(devices - 1)]
        down = [(j, i) for i, j in up]
        last = lax.slice_in_dim(value, length - width, length, axis=dim)
        initial = lax.slice_in_dim(value, 0, width, axis=dim)
        before = lax.ppermute(last, axis, up)
        after = lax.ppermute(initial, axis, down)
        value = jnp.concatenate([before, value, after], axis=dim)
    return value


def gather_rows(value, axis):
    devices = lax.axis_size(axis)
    pieces = [value]
    for shift in range(1, devices):
        pairs = [(i, (i + shift) % devices) for i in range(devices)]
        pieces.append(lax.ppermute(value, axis, pairs))
    return jnp.concatenate(pieces, axis=0)


def layer_norm(value, gain, shift):
    mean = jnp.mean(value, axis=-1, keepdims=True)
    centered = value - mean
    var = jnp.mean(centered * centered, axis=-1, keepdims=True)
    return centered * lax.rsqrt(var + 1e-06) * gain + shift


KV_BLOCK = 4096
LANES = 128


def attend_kernel(q_ref, rn_ref, w_ref, b_ref, m_in_ref, l_in_ref, acc_in_ref, m_ref, l_ref, acc_ref):
    step = pl.program_id(0)
    heads = q_ref.shape[0]
    groups = w_ref.shape[0]

    @pl.when(step == 0)
    def _():
        m_ref[...] = m_in_ref[...]
        l_ref[...] = l_in_ref[...]
        acc_ref[...] = acc_in_ref[...]

    rn = rn_ref[...]

    def one_head(h, keys, values):
        scores = lax.dot_general(
            q_ref[h], keys, (((1,), (1,)), ((), ())), preferred_element_type=jnp.float32
        )
        run_max = m_ref[h]
        new_max = jnp.maximum(run_max, jnp.max(scores, axis=-1, keepdims=True))
        factor = jnp.exp(run_max - new_max)
        expo = jnp.exp(scores - new_max)
        l_ref[h] = l_ref[h] * factor + jnp.sum(expo, axis=-1, keepdims=True)
        acc_ref[h] = acc_ref[h] * factor + jnp.dot(
            expo.astype(jnp.bfloat16), values, preferred_element_type=jnp.float32
        )
        m_ref[h] = new_max

    def project(g):
        projected = (
            jnp.dot(rn, w_ref[g], preferred_element_type=jnp.float32) + b_ref[g]
        ).astype(jnp.bfloat16)
        return projected[:, :LANES], projected[:, LANES:]

    def pair(g, carry):
        keys, values = project(g)
        one_head(2 * g, keys, values)
        one_head(2 * g + 1, keys, values)
        return carry

    lax.fori_loop(0, heads // 2, pair, 0)
    if heads % 2:
        keys, values = project(groups - 1)
        one_head(heads - 1, keys, values)


def attend_part(query_heads, part, weights, bias, state):
    heads, count, lanes = query_heads.shape
    length, chans = part.shape
    column = pl.BlockSpec((heads, count, 1), lambda j: (0, 0, 0))
    whole = pl.BlockSpec((heads, count, lanes), lambda j: (0, 0, 0))
    return pl.pallas_call(
        attend_kernel,
        grid=(length // KV_BLOCK,),
        in_specs=[
            whole,
            pl.BlockSpec((KV_BLOCK, chans), lambda j: (j, 0)),
            pl.BlockSpec(weights.shape, lambda j: (0, 0, 0)),
            pl.BlockSpec(bias.shape, lambda j: (0, 0, 0)),
            column,
            column,
            whole,
        ],
        out_specs=[column, column, whole],
        out_shape=[jax.ShapeDtypeStruct(x.shape, jnp.float32) for x in state],
        compiler_params=pltpu.CompilerParams(
            dimension_semantics=("arbitrary",), vmem_limit_bytes=60 * 1024 * 1024
        ),
    )(query_heads, part, weights, bias, *state)


def attend(query, parts, w_key, w_value, b_value):
    count, chans = query.shape
    head_dim = chans // HEADS
    groups = (HEADS + 1) // 2
    spare = 2 * groups * head_dim - chans

    def by_group(w):
        w = jnp.pad(w, ((0, 0), (0, spare)))
        return w.reshape(chans, groups, LANES).transpose(1, 0, 2)

    weights = jnp.concatenate([by_group(w_key), by_group(w_value)], axis=2)
    value_bias = jnp.pad(b_value, (0, spare)).reshape(groups, LANES)
    bias = jnp.concatenate([jnp.zeros((groups, LANES), jnp.float32), value_bias], axis=1)
    bias = bias.reshape(groups, 1, 2 * LANES)
    query_heads = query.reshape(count, HEADS, head_dim).transpose(1, 0, 2)
    odd = jnp.arange(HEADS) % 2 == 1
    query_heads = jnp.where(
        odd[:, None, None],
        jnp.pad(query_heads, ((0, 0), (0, 0), (head_dim, 0))),
        jnp.pad(query_heads, ((0, 0), (0, 0), (0, head_dim))),
    )
    state = (
        jnp.full((HEADS, count, 1), -1e30, jnp.float32),
        jnp.zeros((HEADS, count, 1), jnp.float32),
        jnp.zeros((HEADS, count, LANES), jnp.float32),
    )
    for part in parts:
        state = attend_part(query_heads, part, weights, bias, state)
    run_max, run_sum, accum = state
    accum = jnp.where(odd[:, None, None], accum[:, :, head_dim:], accum[:, :, :head_dim])
    out = (accum / run_sum).astype(jnp.bfloat16)
    return out.transpose(1, 0, 2).reshape(count, chans)


def per_device(
    tokens,
    norm1_gain,
    norm1_shift,
    w_query,
    b_query,
    w_reduce,
    b_reduce,
    reduce_gain,
    reduce_shift,
    w_key,
    w_value,
    b_value,
    w_out,
    b_out,
    norm2_gain,
    norm2_shift,
    w_expand,
    b_expand,
    w_depth,
    b_depth,
    w_shrink,
    b_shrink,
):
    tile_r, tile_c, chans = tokens.shape
    head_dim = chans // HEADS
    count = tile_r * tile_c
    flat = tokens.reshape(count, chans).astype(jnp.float32)
    normed = layer_norm(flat, norm1_gain, norm1_shift).astype(jnp.bfloat16)
    query = (
        (jnp.dot(normed, w_query, preferred_element_type=jnp.float32) + b_query)
        * head_dim ** (-0.5)
    ).astype(jnp.bfloat16)
    blocks = (
        normed.reshape(tile_r // 2, 2, tile_c // 2, 2, chans)
        .transpose(0, 2, 1, 3, 4)
        .reshape(-1, 4 * chans)
    )
    reduced = jnp.dot(blocks, w_reduce, preferred_element_type=jnp.float32) + b_reduce
    reduced_norm = layer_norm(reduced, reduce_gain, reduce_shift).astype(jnp.bfloat16)

    gathered = gather_rows(reduced_norm, "rows")
    half = gathered.shape[0] // 2
    parts = [
        lax.all_gather(gathered[:half], "cols", axis=0, tiled=True),
        lax.all_gather(gathered[half:], "cols", axis=0, tiled=True),
    ]
    attended = attend(query, parts, w_key, w_value, b_value)
    mid = (flat + jnp.dot(attended, w_out, preferred_element_type=jnp.float32) + b_out).astype(
        jnp.bfloat16
    )
    normed2 = layer_norm(mid.astype(jnp.float32), norm2_gain, norm2_shift).astype(jnp.bfloat16)
    ffn = w_expand.shape[1]
    expanded = (jnp.dot(normed2, w_expand, preferred_element_type=jnp.float32) + b_expand).astype(
        jnp.bfloat16
    )
    grid = expanded.reshape(tile_r, tile_c, ffn)

    def depthwise(source, out_r, out_c):
        total = 0.0
        for tap_r in range(3):
            for tap_c in range(3):
                total = total + (
                    source[tap_r : tap_r + out_r, tap_c : tap_c + out_c, :].astype(jnp.float32)
                    * w_depth[3 * tap_r + tap_c]
                )
        return total

    local = jnp.pad(grid, ((1, 1), (1, 1), (0, 0)))
    spread = lax.optimization_barrier(depthwise(local, tile_r, tile_c) + b_depth)
    padded = padded_2(grid, (("rows", 0), ("cols", 1)), 1)
    inside = np.zeros((tile_r + 2, tile_c + 2, 1), bool)
    inside[1 : tile_r + 1, 1 : tile_c + 1] = True

    def ring(r0, r1, c0, c1):
        return jnp.where(inside[r0:r1, c0:c1], 0, padded[r0:r1, c0:c1])

    top = depthwise(ring(0, 3, 0, tile_c + 2), 1, tile_c)
    bottom = depthwise(ring(tile_r - 1, tile_r + 2, 0, tile_c + 2), 1, tile_c)
    left = depthwise(ring(1, tile_r + 1, 0, 3), tile_r - 2, 1)
    right = depthwise(ring(1, tile_r + 1, tile_c - 1, tile_c + 2), tile_r - 2, 1)
    spread = (
        spread
        + jnp.pad(top, ((0, tile_r - 1), (0, 0), (0, 0)))
        + jnp.pad(bottom, ((tile_r - 1, 0), (0, 0), (0, 0)))
        + jnp.pad(left, ((1, 1), (0, tile_c - 1), (0, 0)))
        + jnp.pad(right, ((1, 1), (tile_c - 1, 0), (0, 0)))
    )
    activated = jax.nn.gelu(spread, approximate=False).astype(jnp.bfloat16).reshape(count, ffn)
    result = (
        mid.astype(jnp.float32)
        + jnp.dot(activated, w_shrink, preferred_element_type=jnp.float32)
        + b_shrink
    )
    return result.astype(jnp.bfloat16).reshape(tile_r, tile_c, chans)


def solution(mesh):
    placed = (
        P("rows", "cols", None),
        P(),
        P(),
        P(),
        P(),
        P(),
        P(),
        P(),
        P(),
        P(),
        P(),
        P(),
        P(),
        P(),
        P(),
        P(),
        P(),
        P(),
        P(),
        P(),
        P(),
        P(),
    )
    return jax.shard_map(
        per_device, mesh=mesh, in_specs=placed, out_specs=P("rows", "cols", None), check_vma=False
    )
```

```python
import jax
import numpy as np
import jax.numpy as jnp
from jax import lax
from jax.sharding import PartitionSpec as P
from jax.experimental import pallas as pl
from jax.experimental.pallas import tpu as pltpu

HEADS = 5


def padded_2(value, sides, width):
    for axis, dim in sides:
        devices, length = (lax.axis_size(axis), value.shape[dim])
        up = [(i, (i + 1) % devices) for i in range(devices - 1)]
        down = [(j, i) for i, j in up]
        last = lax.slice_in_dim(value, length - width, length, axis=dim)
        initial = lax.slice_in_dim(value, 0, width, axis=dim)
        before = lax.ppermute(last, axis, up)
        after = lax.ppermute(initial, axis, down)
        value = jnp.concatenate([before, value, after], axis=dim)
    return value


def gather_rows(value, axis):
    devices = lax.axis_size(axis)
    pieces = [value]
    for shift in range(1, devices):
        pairs = [(i, (i + shift) % devices) for i in range(devices)]
        pieces.append(lax.ppermute(value, axis, pairs))
    return jnp.concatenate(pieces, axis=0)


def layer_norm(value, gain, shift):
    mean = jnp.mean(value, axis=-1, keepdims=True)
    centered = value - mean
    var = jnp.mean(centered * centered, axis=-1, keepdims=True)
    return centered * lax.rsqrt(var + 1e-06) * gain + shift


KV_BLOCK = 2048
LANES = 128


def attend_kernel(q_ref, rn_ref, w_ref, b_ref, m_in_ref, l_in_ref, acc_in_ref, m_ref, l_ref, acc_ref):
    step = pl.program_id(0)
    heads = q_ref.shape[0]
    groups = w_ref.shape[0]

    @pl.when(step == 0)
    def _():
        m_ref[...] = m_in_ref[...]
        l_ref[...] = l_in_ref[...]
        acc_ref[...] = acc_in_ref[...]

    rn = rn_ref[...]

    def one_head(h, keys, values):
        scores = lax.dot_general(
            q_ref[h], keys, (((1,), (1,)), ((), ())), preferred_element_type=jnp.float32
        )
        run_max = m_ref[h]
        new_max = jnp.maximum(run_max, jnp.max(scores, axis=-1, keepdims=True))
        factor = jnp.exp(run_max - new_max)
        expo = jnp.exp(scores - new_max)
        l_ref[h] = l_ref[h] * factor + jnp.sum(expo, axis=-1, keepdims=True)
        acc_ref[h] = acc_ref[h] * factor + jnp.dot(
            expo.astype(jnp.bfloat16), values, preferred_element_type=jnp.float32
        )
        m_ref[h] = new_max

    def project(g):
        projected = (
            jnp.dot(rn, w_ref[g], preferred_element_type=jnp.float32) + b_ref[g]
        ).astype(jnp.bfloat16)
        return projected[:, :LANES], projected[:, LANES:]

    def pair(g, carry):
        keys, values = project(g)
        one_head(2 * g, keys, values)
        one_head(2 * g + 1, keys, values)
        return carry

    lax.fori_loop(0, heads // 2, pair, 0)
    if heads % 2:
        keys, values = project(groups - 1)
        one_head(heads - 1, keys, values)


def attend_part(query_heads, part, weights, bias, state):
    heads, count, lanes = query_heads.shape
    length, chans = part.shape
    column = pl.BlockSpec((heads, count, 1), lambda j: (0, 0, 0))
    whole = pl.BlockSpec((heads, count, lanes), lambda j: (0, 0, 0))
    return pl.pallas_call(
        attend_kernel,
        grid=(length // KV_BLOCK,),
        in_specs=[
            whole,
            pl.BlockSpec((KV_BLOCK, chans), lambda j: (j, 0)),
            pl.BlockSpec(weights.shape, lambda j: (0, 0, 0)),
            pl.BlockSpec(bias.shape, lambda j: (0, 0, 0)),
            column,
            column,
            whole,
        ],
        out_specs=[column, column, whole],
        out_shape=[jax.ShapeDtypeStruct(x.shape, jnp.float32) for x in state],
        compiler_params=pltpu.CompilerParams(
            dimension_semantics=("arbitrary",), vmem_limit_bytes=60 * 1024 * 1024
        ),
    )(query_heads, part, weights, bias, *state)


def attend(query, parts, w_key, w_value, b_value):
    count, chans = query.shape
    head_dim = chans // HEADS
    groups = (HEADS + 1) // 2
    spare = 2 * groups * head_dim - chans

    def by_group(w):
        w = jnp.pad(w, ((0, 0), (0, spare)))
        return w.reshape(chans, groups, LANES).transpose(1, 0, 2)

    weights = jnp.concatenate([by_group(w_key), by_group(w_value)], axis=2)
    value_bias = jnp.pad(b_value, (0, spare)).reshape(groups, LANES)
    bias = jnp.concatenate([jnp.zeros((groups, LANES), jnp.float32), value_bias], axis=1)
    bias = bias.reshape(groups, 1, 2 * LANES)
    query_heads = query.reshape(count, HEADS, head_dim).transpose(1, 0, 2)
    odd = jnp.arange(HEADS) % 2 == 1
    query_heads = jnp.where(
        odd[:, None, None],
        jnp.pad(query_heads, ((0, 0), (0, 0), (head_dim, 0))),
        jnp.pad(query_heads, ((0, 0), (0, 0), (0, head_dim))),
    )
    state = (
        jnp.full((HEADS, count, 1), -1e30, jnp.float32),
        jnp.zeros((HEADS, count, 1), jnp.float32),
        jnp.zeros((HEADS, count, LANES), jnp.float32),
    )
    for part in parts:
        state = attend_part(query_heads, part, weights, bias, state)
    run_max, run_sum, accum = state
    accum = jnp.where(odd[:, None, None], accum[:, :, head_dim:], accum[:, :, :head_dim])
    out = (accum / run_sum).astype(jnp.bfloat16)
    return out.transpose(1, 0, 2).reshape(count, chans)


def per_device(
    tokens,
    norm1_gain,
    norm1_shift,
    w_query,
    b_query,
    w_reduce,
    b_reduce,
    reduce_gain,
    reduce_shift,
    w_key,
    w_value,
    b_value,
    w_out,
    b_out,
    norm2_gain,
    norm2_shift,
    w_expand,
    b_expand,
    w_depth,
    b_depth,
    w_shrink,
    b_shrink,
):
    tile_r, tile_c, chans = tokens.shape
    head_dim = chans // HEADS
    count = tile_r * tile_c
    flat = tokens.reshape(count, chans).astype(jnp.float32)
    normed = layer_norm(flat, norm1_gain, norm1_shift).astype(jnp.bfloat16)
    query = (
        (jnp.dot(normed, w_query, preferred_element_type=jnp.float32) + b_query)
        * head_dim ** (-0.5)
    ).astype(jnp.bfloat16)
    blocks = (
        normed.reshape(tile_r // 2, 2, tile_c // 2, 2, chans)
        .transpose(0, 2, 1, 3, 4)
        .reshape(-1, 4 * chans)
    )
    reduced = jnp.dot(blocks, w_reduce, preferred_element_type=jnp.float32) + b_reduce
    reduced_norm = layer_norm(reduced, reduce_gain, reduce_shift).astype(jnp.bfloat16)

    gathered = gather_rows(reduced_norm, "rows")
    half = gathered.shape[0] // 2
    parts = [
        lax.all_gather(gathered[:half], "cols", axis=0, tiled=True),
        lax.all_gather(gathered[half:], "cols", axis=0, tiled=True),
    ]
    attended = attend(query, parts, w_key, w_value, b_value)
    mid = (flat + jnp.dot(attended, w_out, preferred_element_type=jnp.float32) + b_out).astype(
        jnp.bfloat16
    )
    normed2 = layer_norm(mid.astype(jnp.float32), norm2_gain, norm2_shift).astype(jnp.bfloat16)
    ffn = w_expand.shape[1]
    expanded = (jnp.dot(normed2, w_expand, preferred_element_type=jnp.float32) + b_expand).astype(
        jnp.bfloat16
    )
    grid = expanded.reshape(tile_r, tile_c, ffn)

    def depthwise(source, out_r, out_c):
        total = 0.0
        for tap_r in range(3):
            for tap_c in range(3):
                total = total + (
                    source[tap_r : tap_r + out_r, tap_c : tap_c + out_c, :].astype(jnp.float32)
                    * w_depth[3 * tap_r + tap_c]
                )
        return total

    local = jnp.pad(grid, ((1, 1), (1, 1), (0, 0)))
    spread = lax.optimization_barrier(depthwise(local, tile_r, tile_c) + b_depth)
    padded = padded_2(grid, (("rows", 0), ("cols", 1)), 1)
    inside = np.zeros((tile_r + 2, tile_c + 2, 1), bool)
    inside[1 : tile_r + 1, 1 : tile_c + 1] = True

    def ring(r0, r1, c0, c1):
        return jnp.where(inside[r0:r1, c0:c1], 0, padded[r0:r1, c0:c1])

    top = depthwise(ring(0, 3, 0, tile_c + 2), 1, tile_c)
    bottom = depthwise(ring(tile_r - 1, tile_r + 2, 0, tile_c + 2), 1, tile_c)
    left = depthwise(ring(1, tile_r + 1, 0, 3), tile_r - 2, 1)
    right = depthwise(ring(1, tile_r + 1, tile_c - 1, tile_c + 2), tile_r - 2, 1)
    spread = (
        spread
        + jnp.pad(top, ((0, tile_r - 1), (0, 0), (0, 0)))
        + jnp.pad(bottom, ((tile_r - 1, 0), (0, 0), (0, 0)))
        + jnp.pad(left, ((1, 1), (0, tile_c - 1), (0, 0)))
        + jnp.pad(right, ((1, 1), (tile_c - 1, 0), (0, 0)))
    )
    activated = jax.nn.gelu(spread, approximate=False).astype(jnp.bfloat16).reshape(count, ffn)
    result = (
        mid.astype(jnp.float32)
        + jnp.dot(activated, w_shrink, preferred_element_type=jnp.float32)
        + b_shrink
    )
    return result.astype(jnp.bfloat16).reshape(tile_r, tile_c, chans)


def solution(mesh):
    placed = (
        P("rows", "cols", None),
        P(),
        P(),
        P(),
        P(),
        P(),
        P(),
        P(),
        P(),
        P(),
        P(),
        P(),
        P(),
        P(),
        P(),
        P(),
        P(),
        P(),
        P(),
        P(),
        P(),
        P(),
    )
    return jax.shard_map(
        per_device, mesh=mesh, in_specs=placed, out_specs=P("rows", "cols", None), check_vma=False
    )
```

```python
import jax
import numpy as np
import jax.numpy as jnp
from jax import lax
from jax.sharding import PartitionSpec as P
from jax.experimental import pallas as pl
from jax.experimental.pallas import tpu as pltpu

HEADS = 5


def padded_2(value, sides, width):
    for axis, dim in sides:
        devices, length = (lax.axis_size(axis), value.shape[dim])
        up = [(i, (i + 1) % devices) for i in range(devices - 1)]
        down = [(j, i) for i, j in up]
        last = lax.slice_in_dim(value, length - width, length, axis=dim)
        initial = lax.slice_in_dim(value, 0, width, axis=dim)
        before = lax.ppermute(last, axis, up)
        after = lax.ppermute(initial, axis, down)
        value = jnp.concatenate([before, value, after], axis=dim)
    return value


def gather_rows(value, axis):
    devices = lax.axis_size(axis)
    pieces = [value]
    for shift in range(1, devices):
        pairs = [(i, (i + shift) % devices) for i in range(devices)]
        pieces.append(lax.ppermute(value, axis, pairs))
    return jnp.concatenate(pieces, axis=0)


def layer_norm(value, gain, shift):
    mean = jnp.mean(value, axis=-1, keepdims=True)
    centered = value - mean
    var = jnp.mean(centered * centered, axis=-1, keepdims=True)
    return centered * lax.rsqrt(var + 1e-06) * gain + shift


KV_BLOCK = 4096
LANES = 128


def attend_kernel(q_ref, rn_ref, w_ref, b_ref, *refs):
    step = pl.program_id(0)
    heads = q_ref.shape[0]
    groups = w_ref.shape[0]
    m_ref, l_ref, acc_ref = refs[-3:]

    @pl.when(step == 0)
    def _():
        if len(refs) == 6:
            m_ref[...] = refs[0][...]
            l_ref[...] = refs[1][...]
            acc_ref[...] = refs[2][...]
        else:
            m_ref[...] = jnp.full(m_ref.shape, -1e30, jnp.float32)
            l_ref[...] = jnp.zeros(l_ref.shape, jnp.float32)
            acc_ref[...] = jnp.zeros(acc_ref.shape, jnp.float32)

    rn = rn_ref[...]

    def one_head(h, keys, values):
        scores = lax.dot_general(
            q_ref[h], keys, (((1,), (1,)), ((), ())), preferred_element_type=jnp.float32
        )
        run_max = m_ref[h]
        new_max = jnp.maximum(run_max, jnp.max(scores, axis=-1, keepdims=True))
        factor = jnp.exp(run_max - new_max)
        expo = jnp.exp(scores - new_max)
        l_ref[h] = l_ref[h] * factor + jnp.sum(expo, axis=-1, keepdims=True)
        acc_ref[h] = acc_ref[h] * factor + jnp.dot(
            expo.astype(jnp.bfloat16), values, preferred_element_type=jnp.float32
        )
        m_ref[h] = new_max

    def project(g):
        projected = (
            jnp.dot(rn, w_ref[g], preferred_element_type=jnp.float32) + b_ref[g]
        ).astype(jnp.bfloat16)
        return projected[:, :LANES], projected[:, LANES:]

    def pair(g, carry):
        keys, values = project(g)
        one_head(2 * g, keys, values)
        one_head(2 * g + 1, keys, values)
        return carry

    lax.fori_loop(0, heads // 2, pair, 0)
    if heads % 2:
        keys, values = project(groups - 1)
        one_head(heads - 1, keys, values)


def attend_part(query_heads, part, weights, bias, state):
    heads, count, lanes = query_heads.shape
    length, chans = part.shape
    column = pl.BlockSpec((heads, count, 1), lambda j: (0, 0, 0))
    whole = pl.BlockSpec((heads, count, lanes), lambda j: (0, 0, 0))
    return pl.pallas_call(
        attend_kernel,
        grid=(length // KV_BLOCK,),
        in_specs=[
            whole,
            pl.BlockSpec((KV_BLOCK, chans), lambda j: (j, 0)),
            pl.BlockSpec(weights.shape, lambda j: (0, 0, 0)),
            pl.BlockSpec(bias.shape, lambda j: (0, 0, 0)),
        ]
        + [column, column, whole][: len(state)],
        out_specs=[column, column, whole],
        out_shape=[
            jax.ShapeDtypeStruct((heads, count, 1), jnp.float32),
            jax.ShapeDtypeStruct((heads, count, 1), jnp.float32),
            jax.ShapeDtypeStruct((heads, count, lanes), jnp.float32),
        ],
        compiler_params=pltpu.CompilerParams(
            dimension_semantics=("arbitrary",), vmem_limit_bytes=60 * 1024 * 1024
        ),
    )(query_heads, part, weights, bias, *state)


def attend(query, parts, w_key, w_value, b_value):
    count, chans = query.shape
    head_dim = chans // HEADS
    groups = (HEADS + 1) // 2
    spare = 2 * groups * head_dim - chans

    def by_group(w):
        w = jnp.pad(w, ((0, 0), (0, spare)))
        return w.reshape(chans, groups, LANES).transpose(1, 0, 2)

    weights = jnp.concatenate([by_group(w_key), by_group(w_value)], axis=2)
    value_bias = jnp.pad(b_value, (0, spare)).reshape(groups, LANES)
    bias = jnp.concatenate([jnp.zeros((groups, LANES), jnp.float32), value_bias], axis=1)
    bias = bias.reshape(groups, 1, 2 * LANES)
    query_heads = query.reshape(count, HEADS, head_dim).transpose(1, 0, 2)
    odd = jnp.arange(HEADS) % 2 == 1
    query_heads = jnp.where(
        odd[:, None, None],
        jnp.pad(query_heads, ((0, 0), (0, 0), (head_dim, 0))),
        jnp.pad(query_heads, ((0, 0), (0, 0), (0, head_dim))),
    )
    state = ()
    for part in parts:
        state = attend_part(query_heads, part, weights, bias, state)
    run_max, run_sum, accum = state
    accum = jnp.where(odd[:, None, None], accum[:, :, head_dim:], accum[:, :, :head_dim])
    out = (accum / run_sum).astype(jnp.bfloat16)
    return out.transpose(1, 0, 2).reshape(count, chans)


def per_device(
    tokens,
    norm1_gain,
    norm1_shift,
    w_query,
    b_query,
    w_reduce,
    b_reduce,
    reduce_gain,
    reduce_shift,
    w_key,
    w_value,
    b_value,
    w_out,
    b_out,
    norm2_gain,
    norm2_shift,
    w_expand,
    b_expand,
    w_depth,
    b_depth,
    w_shrink,
    b_shrink,
):
    tile_r, tile_c, chans = tokens.shape
    head_dim = chans // HEADS
    count = tile_r * tile_c
    flat = tokens.reshape(count, chans).astype(jnp.float32)
    normed = layer_norm(flat, norm1_gain, norm1_shift).astype(jnp.bfloat16)
    query = (
        (jnp.dot(normed, w_query, preferred_element_type=jnp.float32) + b_query)
        * head_dim ** (-0.5)
    ).astype(jnp.bfloat16)
    blocks = (
        normed.reshape(tile_r // 2, 2, tile_c // 2, 2, chans)
        .transpose(0, 2, 1, 3, 4)
        .reshape(-1, 4 * chans)
    )
    reduced = jnp.dot(blocks, w_reduce, preferred_element_type=jnp.float32) + b_reduce
    reduced_norm = layer_norm(reduced, reduce_gain, reduce_shift).astype(jnp.bfloat16)

    gathered = gather_rows(reduced_norm, "rows")
    half = gathered.shape[0] // 2
    parts = [
        lax.all_gather(gathered[:half], "cols", axis=0, tiled=True),
        lax.all_gather(gathered[half:], "cols", axis=0, tiled=True),
    ]
    attended = attend(query, parts, w_key, w_value, b_value)
    mid = (flat + jnp.dot(attended, w_out, preferred_element_type=jnp.float32) + b_out).astype(
        jnp.bfloat16
    )
    normed2 = layer_norm(mid.astype(jnp.float32), norm2_gain, norm2_shift).astype(jnp.bfloat16)
    ffn = w_expand.shape[1]
    expanded = (jnp.dot(normed2, w_expand, preferred_element_type=jnp.float32) + b_expand).astype(
        jnp.bfloat16
    )
    grid = expanded.reshape(tile_r, tile_c, ffn)

    def depthwise(source, out_r, out_c):
        total = 0.0
        for tap_r in range(3):
            for tap_c in range(3):
                total = total + (
                    source[tap_r : tap_r + out_r, tap_c : tap_c + out_c, :].astype(jnp.float32)
                    * w_depth[3 * tap_r + tap_c]
                )
        return total

    local = jnp.pad(grid, ((1, 1), (1, 1), (0, 0)))
    spread = lax.optimization_barrier(depthwise(local, tile_r, tile_c) + b_depth)
    padded = padded_2(grid, (("rows", 0), ("cols", 1)), 1)
    inside = np.zeros((tile_r + 2, tile_c + 2, 1), bool)
    inside[1 : tile_r + 1, 1 : tile_c + 1] = True

    def ring(r0, r1, c0, c1):
        return jnp.where(inside[r0:r1, c0:c1], 0, padded[r0:r1, c0:c1])

    top = depthwise(ring(0, 3, 0, tile_c + 2), 1, tile_c)
    bottom = depthwise(ring(tile_r - 1, tile_r + 2, 0, tile_c + 2), 1, tile_c)
    left = depthwise(ring(1, tile_r + 1, 0, 3), tile_r - 2, 1)
    right = depthwise(ring(1, tile_r + 1, tile_c - 1, tile_c + 2), tile_r - 2, 1)
    spread = (
        spread
        + jnp.pad(top, ((0, tile_r - 1), (0, 0), (0, 0)))
        + jnp.pad(bottom, ((tile_r - 1, 0), (0, 0), (0, 0)))
        + jnp.pad(left, ((1, 1), (0, tile_c - 1), (0, 0)))
        + jnp.pad(right, ((1, 1), (tile_c - 1, 0), (0, 0)))
    )
    activated = jax.nn.gelu(spread, approximate=False).astype(jnp.bfloat16).reshape(count, ffn)
    result = (
        mid.astype(jnp.float32)
        + jnp.dot(activated, w_shrink, preferred_element_type=jnp.float32)
        + b_shrink
    )
    return result.astype(jnp.bfloat16).reshape(tile_r, tile_c, chans)


def solution(mesh):
    placed = (
        P("rows", "cols", None),
        P(),
        P(),
        P(),
        P(),
        P(),
        P(),
        P(),
        P(),
        P(),
        P(),
        P(),
        P(),
        P(),
        P(),
        P(),
        P(),
        P(),
        P(),
        P(),
        P(),
        P(),
    )
    return jax.shard_map(
        per_device, mesh=mesh, in_specs=placed, out_specs=P("rows", "cols", None), check_vma=False
    )
```
